256 devices in a mesh: space: 128 (over z, y, x), rep: 2 (over core).
Axes of the slice: x: 4, y: 4, z: 8, core: 2. Of those that a mesh axis runs over, the one named last changes fastest.
Arguments:
- features: bfloat16 [2, 256, 512, 128], P('rep', 'space'), may hold values from -6 to 6
- voxel_mask: int32 [2, 256, 512], P('rep', 'space'), may hold values from 0 to 1, as said below
- neighbours: int32 [2, 256, 27], P('rep', 'space'), may hold values from 0 to 34, as said below
- send_slots: int32 [2, 2048], P('rep', 'space'), may hold values from 0 to 2, as said below
- w_sub: bfloat16 [27, 128, 128], replicated, may hold values from -0.109375 to 0.109375
- w_down: bfloat16 [8, 128, 256], replicated, may hold values from -0.1875 to 0.1875
- cotangent: bfloat16 [2, 256, 64, 256], P('rep', 'space'), may hold values from -6 to 6
Outputs:
- coarse: bfloat16 [2, 256, 64, 256], P('rep', 'space')
- grad_feats: bfloat16 [2, 256, 512, 128], P('rep', 'space')
- grad_sub: float32 [27, 128, 128], replicated
- grad_down: float32 [8, 128, 256], replicated
The draws below stay inside these ranges and needn't reach their ends.
Inputs may be any that keep to these rules, and one draw needn't show every extreme that they name: `voxel_mask`: 0 or 1. Each slab of a scan has 1 or 2 live slots, and these are the lowest-numbered ones; some slab of each scan has 2 live slots; all voxels of slots that are not live are 0. `neighbours`: each live slot holds one brick position (p1, p2) of its slab s, p = 4 p1 + p2, one brick per position; its brick neighbour at offset (a, b, c) lies at slab s + a, position (p1 + b, p2 + c). Entry: its slot if a = 0 and that position is live, 2 + p' if a = -1, 18 + p' if a = 1, where p' is the neighbour's position; 34 where the neighbour lies outside the map or is empty on the own slab, and for every offset of a slot that is not live. `send_slots`: entry p of slab s is the slot holding position p, or 2 where no live slot holds it.
All inputs are finite; a program needn't handle non-finite values.
Results may differ from the reference program's by a relative error of at most 0.015.
Values may be sent and summed in bfloat16 or wider, within the bound.
No kernel may reach another device: no remote copies, remote signals or barrier semaphores. Data moves between devices by JAX's collectives and lax.ppermute only.
A program may use at most 128 MiB of HBM per device.

```python
import jax
import jax.numpy as jnp
from jax import lax

C = 128
C2 = 256
VOX = 512
SIDE = 4
BRK_DEV = 2
CELLS = 16
SCANS = 2
BRICKS = 256
N_SPACE = 128


def layout(key):
    base = jax.random.fold_in(key, 17)
    key_count, key_peak, key_order = jax.random.split(base, 3)
    least_count = max(1, BRK_DEV * 3 // 4)
    counts = jax.random.randint(key_count, (SCANS, N_SPACE), least_count, BRK_DEV + 1)
    peak_index = jax.random.randint(key_peak, (SCANS, 1), 0, N_SPACE)
    counts = jnp.where(jnp.arange(N_SPACE)[None, :] == peak_index, BRK_DEV, counts).astype(jnp.int32)
    scores = jax.random.randint(key_order, (SCANS, N_SPACE, CELLS), 0, 1048576) * CELLS + jnp.arange(CELLS)[None, None, :]
    slot_cell = jnp.argsort(scores, axis=-1).astype(jnp.int32)
    cell_slot = jnp.argsort(slot_cell, axis=-1).astype(jnp.int32)
    return (counts, slot_cell, cell_slot)


def draw_voxel_mask(key, part):
    counts, slot_cell, cell_slot = layout(key)
    voxel_key = jax.random.fold_in(key, 29)
    filled = jax.random.randint(voxel_key, (SCANS, N_SPACE, BRK_DEV, VOX), 0, 5) < 4
    live_slot = jnp.arange(BRK_DEV)[None, None, :] < counts[:, :, None]
    return (filled & live_slot[..., None]).astype(jnp.int32).reshape(SCANS, BRICKS, VOX)


def draw_send_slots(key, part):
    counts, slot_cell, cell_slot = layout(key)
    live_cell = cell_slot < counts[:, :, None]
    chosen = jnp.where(live_cell, cell_slot, BRK_DEV)
    return chosen.astype(jnp.int32).reshape(SCANS, N_SPACE * CELLS)


def draw_neighbours(key, part):
    counts, slot_cell, cell_slot = layout(key)
    empty_row = BRK_DEV + 2 * CELLS
    cell_pos = slot_cell[:, :, :BRK_DEV]
    cell_y = cell_pos // SIDE
    cell_z = cell_pos % SIDE
    direction = jnp.arange(27)
    step_x = direction // 9 - 1
    step_y = direction // 3 % 3 - 1
    step_z = direction % 3 - 1
    new_y = cell_y[..., None] + step_y
    new_z = cell_z[..., None] + step_z
    inside = (new_y >= 0) & (new_y < SIDE) & (new_z >= 0) & (new_z < SIDE)
    target = jnp.clip(new_y, 0, SIDE - 1) * SIDE + jnp.clip(new_z, 0, SIDE - 1)
    local_slot = jnp.take_along_axis(cell_slot, target.reshape(SCANS, N_SPACE, BRK_DEV * 27), axis=2).reshape(SCANS, N_SPACE, BRK_DEV, 27)
    from_local = jnp.where(local_slot < counts[:, :, None, None], local_slot, empty_row)
    device = jnp.arange(N_SPACE)[None, :, None, None]
    from_lower = jnp.where(device > 0, BRK_DEV + target, empty_row)
    from_upper = jnp.where(device < N_SPACE - 1, BRK_DEV + CELLS + target, empty_row)
    chosen = jnp.where(step_x == -1, from_lower, jnp.where(step_x == 0, from_local, from_upper))
    chosen = jnp.where(inside, chosen, empty_row)
    live_slot = jnp.arange(BRK_DEV)[None, None, :, None] < counts[:, :, None, None]
    chosen = jnp.where(live_slot, chosen, empty_row)
    return chosen.astype(jnp.int32).reshape(SCANS, BRICKS, 27)


def level_of(stream_key, shape, cuts, smallest, largest):
    def one(dim, parts):
        steps = jax.random.uniform(jax.random.fold_in(jax.random.fold_in(stream_key, 6), dim), (parts,), jnp.float32, smallest / len(cuts), largest / len(cuts))
        return jnp.repeat(jnp.exp(steps), shape[dim] // parts).reshape((-1,) + (1,) * (len(shape) - dim - 1))

    level = one(*cuts[0])
    for cut in cuts[1:]:
        level = level * one(*cut)
    return level


def noise(key, shape, deviation, bound, cuts=(), kind=jnp.bfloat16):
    values = deviation * jax.random.normal(key, shape, jnp.float32)
    if cuts:
        values = values * level_of(key, shape, cuts, -0.22, 0.18)
    return jnp.clip(values, -bound, bound).astype(kind)


def setup_inputs(seed: int = 0) -> dict:
    key_of = jax.random.split(jax.random.key(seed), 8)
    return {
        "features": noise(key_of[0], (SCANS, BRICKS, VOX, C), 1.0, 6.0, ((0, 2), (1, 128))),
        "voxel_mask": draw_voxel_mask(jax.random.fold_in(key_of[7], 71), 0),
        "neighbours": draw_neighbours(jax.random.fold_in(key_of[7], 71), 0),
        "send_slots": draw_send_slots(jax.random.fold_in(key_of[7], 71), 0),
        "w_sub": noise(key_of[4], (27, C, C), (27 * C) ** -0.5, 0.109375),
        "w_down": noise(key_of[5], (8, C, C2), (8 * C) ** -0.5, 0.1875),
        "cotangent": noise(key_of[6], (SCANS, BRICKS, VOX // 8, C2), 1.0, 6.0, ((0, 2), (1, 128))),
    }


def extent(shift):
    if shift < 0:
        return (7, 8)
    if shift == 0:
        return (0, 8)
    return (0, 1)

def pad_bricks(lookup, link_rows):
    planes = []
    for shift_x in (-1, 0, 1):
        row_parts = []
        for shift_y in (-1, 0, 1):
            cell_parts = []
            for shift_z in (-1, 0, 1):
                column = (shift_x + 1) * 9 + (shift_y + 1) * 3 + (shift_z + 1)
                low_x, high_x = extent(shift_x)
                low_y, high_y = extent(shift_y)
                low_z, high_z = extent(shift_z)
                section = lookup[:, low_x:high_x, low_y:high_y, low_z:high_z]
                cell_parts.append(jnp.take(section, link_rows[:, column], axis=0))
            row_parts.append(jnp.concatenate(cell_parts, axis=3))
        planes.append(jnp.concatenate(row_parts, axis=2))
    return jnp.concatenate(planes, axis=1)

def conv_forward(padded, w_sub):
    channels = padded.shape[-1]
    running = jnp.zeros((padded.shape[0] * 512, w_sub.shape[2]), jnp.float32)
    for offset in range(27):
        start_x, start_y, start_z = (offset // 9, offset // 3 % 3, offset % 3)
        window = padded[:, start_x:start_x + 8, start_y:start_y + 8, start_z:start_z + 8].reshape(-1, channels)
        running = running + jnp.dot(window, w_sub[offset], preferred_element_type=jnp.float32)
    return running

def conv_transpose(padded, w_sub):
    channels = padded.shape[-1]
    running = jnp.zeros((padded.shape[0] * 512, w_sub.shape[1]), jnp.float32)
    for offset in range(27):
        start_x, start_y, start_z = (2 - offset // 9, 2 - offset // 3 % 3, 2 - offset % 3)
        window = padded[:, start_x:start_x + 8, start_y:start_y + 8, start_z:start_z + 8].reshape(-1, channels)
        running = running + jnp.dot(window, w_sub[offset].T, preferred_element_type=jnp.float32)
    return running

def weight_grad(padded, grad_rows):
    channels = padded.shape[-1]
    results = []
    for offset in range(27):
        start_x, start_y, start_z = (offset // 9, offset // 3 % 3, offset % 3)
        window = padded[:, start_x:start_x + 8, start_y:start_y + 8, start_z:start_z + 8].reshape(-1, channels)
        results.append(lax.dot_general(window, grad_rows, (((0,), (0,)), ((), ())), preferred_element_type=jnp.float32))
    return jnp.stack(results)

def to_columns(values):
    bricks = values.shape[0]
    channels = values.shape[-1]
    cube = values.reshape(bricks, 4, 2, 4, 2, 4, 2, channels)
    return cube.transpose(0, 1, 3, 5, 2, 4, 6, 7).reshape(bricks * 64, 8 * channels)

def from_columns(columns, bricks, channels):
    cube = columns.reshape(bricks, 4, 4, 4, 2, 2, 2, channels)
    return cube.transpose(0, 1, 4, 2, 5, 3, 6, 7).reshape(bricks, 512, channels)

def silu_slope(values):
    sigmoid_value = jax.nn.sigmoid(values)
    return sigmoid_value * (1.0 + values * (1.0 - sigmoid_value))

def pick_row(array, index):
    return lax.dynamic_index_in_dim(array, index, 0, keepdims=False)

def send_rows(values, slots):
    zero_row = jnp.zeros((1,) + values.shape[1:], values.dtype)
    return jnp.take(jnp.concatenate([values, zero_row], axis=0), slots, axis=0)

def device_table(values_all, slots_all, device):
    channels = values_all.shape[-1]
    own_bricks = pick_row(values_all, device)
    lower_index = jnp.maximum(device - 1, 0)
    upper_index = jnp.minimum(device + 1, N_SPACE - 1)
    lower_rows = send_rows(pick_row(values_all, lower_index), pick_row(slots_all, lower_index))
    lower_rows = jnp.where(device > 0, lower_rows, jnp.zeros_like(lower_rows))
    upper_rows = send_rows(pick_row(values_all, upper_index), pick_row(slots_all, upper_index))
    upper_rows = jnp.where(device < N_SPACE - 1, upper_rows, jnp.zeros_like(upper_rows))
    zero_row = jnp.zeros((1,) + own_bricks.shape[1:], own_bricks.dtype)
    return jnp.concatenate([own_bricks, lower_rows, upper_rows, zero_row], axis=0).reshape(-1, 8, 8, 8, channels)

def reference(features, voxel_mask, neighbours, send_slots, w_sub, w_down, cotangent):
    channels = features.shape[-1]
    out_channels = w_down.shape[2]
    down_flat = w_down.reshape(-1, out_channels)
    sub_total = jnp.zeros(w_sub.shape, jnp.float32)
    down_total = jnp.zeros(down_flat.shape, jnp.float32)
    coarse_list = []
    grad_list = []
    devices = jnp.arange(N_SPACE, dtype=jnp.int32)
    for scan_index in range(SCANS):
        occupancy_all = voxel_mask[scan_index].reshape(N_SPACE, BRK_DEV * VOX).astype(jnp.float32)
        masked_all = (features[scan_index] * voxel_mask[scan_index][..., None].astype(jnp.bfloat16)).reshape(N_SPACE, BRK_DEV, VOX, channels)
        slots_all = send_slots[scan_index].reshape(N_SPACE, CELLS)
        links_all = neighbours[scan_index].reshape(N_SPACE, BRK_DEV, 27)
        cotangent_all = cotangent[scan_index].reshape(N_SPACE, BRK_DEV * (VOX // 8), out_channels)

        def forward_step(running_sum, device):
            occupancy = pick_row(occupancy_all, device)
            padded = pad_bricks(device_table(masked_all, slots_all, device), pick_row(links_all, device))
            pre_act = conv_forward(padded, w_sub) * occupancy[:, None]
            hidden = jax.nn.silu(pre_act).astype(jnp.bfloat16)
            columns = to_columns(hidden.reshape(BRK_DEV, VOX, channels))
            coarse_mask = lax.optimization_barrier(jnp.max(to_columns(occupancy.reshape(BRK_DEV, VOX, 1)), axis=1))
            coarse = (jnp.dot(columns, down_flat, preferred_element_type=jnp.float32) * coarse_mask[:, None]).astype(jnp.bfloat16)
            grad_coarse = pick_row(cotangent_all, device) * coarse_mask[:, None].astype(jnp.bfloat16)
            grad_cols = jnp.dot(grad_coarse, down_flat.T, preferred_element_type=jnp.float32).astype(jnp.bfloat16)
            grad_hidden = from_columns(grad_cols, BRK_DEV, channels).reshape(-1, channels)
            grad_pre = (grad_hidden.astype(jnp.float32) * silu_slope(pre_act) * occupancy[:, None]).astype(jnp.bfloat16)
            running_sum = running_sum + lax.dot_general(columns, grad_coarse, (((0,), (0,)), ((), ())), preferred_element_type=jnp.float32)
            return (running_sum, (coarse, grad_pre.reshape(BRK_DEV, VOX, channels)))
        down_total, (coarse_all, grad_pre_all) = lax.scan(forward_step, down_total, devices)

        def backward_step(running_sum, device):
            occupancy = pick_row(occupancy_all, device)
            link_rows = pick_row(links_all, device)
            padded_x = pad_bricks(device_table(masked_all, slots_all, device), link_rows)
            padded_g = pad_bricks(device_table(grad_pre_all, slots_all, device), link_rows)
            grad_in = (conv_transpose(padded_g, w_sub) * occupancy[:, None]).astype(jnp.bfloat16)
            grad_rows = pick_row(grad_pre_all, device).reshape(-1, channels)
            running_sum = running_sum + weight_grad(padded_x, grad_rows)
            return (running_sum, grad_in.reshape(BRK_DEV, VOX, channels))
        sub_total, grad_all = lax.scan(backward_step, sub_total, devices)
        coarse_list.append(coarse_all.reshape(BRICKS, VOX // 8, out_channels))
        grad_list.append(grad_all.reshape(BRICKS, VOX, channels))
    inverse_count = 1.0 / (N_SPACE * SCANS)
    return (jnp.stack(coarse_list), jnp.stack(grad_list), sub_total * inverse_count, (down_total * inverse_count).reshape(w_down.shape))
```

```python
import jax
import jax.numpy as jnp
from jax import lax
from jax.sharding import PartitionSpec as P


def from_behind(value, axis, steps):
    count = lax.axis_size(axis)
    leading, last = (max(0, -steps), min(count, count - steps))
    return lax.ppermute(value, axis, [(source, source + steps) for source in range(leading, last)])


def _xor_pairs(count, bit):
    return [(index, index ^ bit) for index in range(count)]


def tree_psum(flat, steps):
    buf = flat
    for axis, bit in steps:
        me = (lax.axis_index(axis) // bit) % 2
        halves = buf.reshape(2, -1)
        keep = lax.dynamic_index_in_dim(halves, me, 0, keepdims=False)
        send = lax.dynamic_index_in_dim(halves, 1 - me, 0, keepdims=False)
        buf = keep + lax.ppermute(send, axis, _xor_pairs(lax.axis_size(axis), bit))
    for axis, bit in reversed(steps):
        me = (lax.axis_index(axis) // bit) % 2
        pair = jnp.stack([buf, lax.ppermute(buf, axis, _xor_pairs(lax.axis_size(axis), bit))])
        first = lax.dynamic_index_in_dim(pair, me, 0, keepdims=False)
        second = lax.dynamic_index_in_dim(pair, 1 - me, 0, keepdims=False)
        buf = jnp.concatenate([first, second])
    return buf


def reduce_steps():
    steps = [("rep", bit) for bit in (1, 2, 4) if bit < lax.axis_size("rep")]
    count = lax.axis_size("space")
    preferred = [1, 4, 16, 2, 8, 32, 64]
    bits = [bit for bit in preferred if bit < count]
    bits += [1 << k for k in range(count.bit_length()) if (1 << k) < count and (1 << k) not in bits]
    return steps + [("space", bit) for bit in bits]


def extent(shift):
    if shift < 0:
        return (7, 8)
    if shift == 0:
        return (0, 8)
    return (0, 1)


def pad_bricks(lookup, link_rows):
    planes = []
    for shift_x in (-1, 0, 1):
        row_parts = []
        for shift_y in (-1, 0, 1):
            cell_parts = []
            for shift_z in (-1, 0, 1):
                column = (shift_x + 1) * 9 + (shift_y + 1) * 3 + (shift_z + 1)
                low_x, high_x = extent(shift_x)
                low_y, high_y = extent(shift_y)
                low_z, high_z = extent(shift_z)
                section = lookup[:, low_x:high_x, low_y:high_y, low_z:high_z]
                cell_parts.append(jnp.take(section, link_rows[:, column], axis=0))
            row_parts.append(jnp.concatenate(cell_parts, axis=3))
        planes.append(jnp.concatenate(row_parts, axis=2))
    return jnp.concatenate(planes, axis=1)


def conv_forward(padded, w_sub):
    channels = padded.shape[-1]
    running = jnp.zeros((padded.shape[0] * 512, w_sub.shape[2]), jnp.float32)
    for offset in range(27):
        start_x, start_y, start_z = (offset // 9, offset // 3 % 3, offset % 3)
        window = padded[
            :, start_x : start_x + 8, start_y : start_y + 8, start_z : start_z + 8
        ].reshape(-1, channels)
        running = running + jnp.dot(window, w_sub[offset], preferred_element_type=jnp.float32)
    return running


def conv_transpose(padded, w_sub):
    channels = padded.shape[-1]
    running = jnp.zeros((padded.shape[0] * 512, w_sub.shape[1]), jnp.float32)
    for offset in range(27):
        start_x, start_y, start_z = (2 - offset // 9, 2 - offset // 3 % 3, 2 - offset % 3)
        window = padded[
            :, start_x : start_x + 8, start_y : start_y + 8, start_z : start_z + 8
        ].reshape(-1, channels)
        running = running + jnp.dot(window, w_sub[offset].T, preferred_element_type=jnp.float32)
    return running


def weight_grad(padded, grad_rows):
    channels = padded.shape[-1]
    results = []
    for offset in range(27):
        start_x, start_y, start_z = (offset // 9, offset // 3 % 3, offset % 3)
        window = padded[
            :, start_x : start_x + 8, start_y : start_y + 8, start_z : start_z + 8
        ].reshape(-1, channels)
        results.append(
            lax.dot_general(
                window, grad_rows, (((0,), (0,)), ((), ())), preferred_element_type=jnp.float32
            )
        )
    return jnp.stack(results)


def to_columns(values):
    bricks = values.shape[0]
    channels = values.shape[-1]
    cube = values.reshape(bricks, 4, 2, 4, 2, 4, 2, channels)
    return cube.transpose(0, 1, 3, 5, 2, 4, 6, 7).reshape(bricks * 64, 8 * channels)


def from_columns(columns, bricks, channels):
    cube = columns.reshape(bricks, 4, 4, 4, 2, 2, 2, channels)
    return cube.transpose(0, 1, 4, 2, 5, 3, 6, 7).reshape(bricks, 512, channels)


def silu_slope(values):
    sigmoid_value = jax.nn.sigmoid(values)
    return sigmoid_value * (1.0 + values * (1.0 - sigmoid_value))


def halo_table(values, send_list):
    bricks = values.shape[0]
    channels = values.shape[-1]
    zero_row = jnp.zeros((1,) + values.shape[1:], values.dtype)
    outgoing = jnp.take(jnp.concatenate([values, zero_row], axis=0), send_list, axis=0)
    cell_count = outgoing.shape[0]
    from_lower = from_behind(outgoing, "space", 1)
    from_upper = from_behind(outgoing, "space", -1)
    lower_blocks = from_lower.reshape(cell_count, 8, 8, 8, channels)
    upper_blocks = from_upper.reshape(cell_count, 8, 8, 8, channels)
    own_bricks = values.reshape(bricks, 8, 8, 8, channels)
    empty_brick = jnp.zeros((1, 8, 8, 8, channels), values.dtype)
    return jnp.concatenate([own_bricks, lower_blocks, upper_blocks, empty_brick], axis=0)


def body(features, voxel_mask, neighbours, send_slots, w_sub, w_down, cotangent):
    values = features[0]
    bricks, voxels, channels = values.shape
    out_channels = w_down.shape[2]
    link_rows = neighbours[0]
    send_list = send_slots[0]
    occupancy = voxel_mask[0].reshape(-1).astype(jnp.float32)
    masked = values * voxel_mask[0][..., None].astype(jnp.bfloat16)
    padded_x = pad_bricks(halo_table(masked, send_list), link_rows)
    pre_act = conv_forward(padded_x, w_sub) * occupancy[:, None]
    hidden = jax.nn.silu(pre_act).astype(jnp.bfloat16)
    columns = to_columns(hidden.reshape(bricks, voxels, channels))
    down_flat = w_down.reshape(-1, out_channels)
    coarse_mask = jnp.max(to_columns(occupancy.reshape(bricks, voxels, 1)), axis=1)
    coarse = (
        jnp.dot(columns, down_flat, preferred_element_type=jnp.float32) * coarse_mask[:, None]
    ).astype(jnp.bfloat16)
    grad_coarse = cotangent[0].reshape(-1, out_channels) * coarse_mask[:, None].astype(jnp.bfloat16)
    grad_cols = jnp.dot(grad_coarse, down_flat.T, preferred_element_type=jnp.float32).astype(
        jnp.bfloat16
    )
    grad_hidden = from_columns(grad_cols, bricks, channels).reshape(-1, channels)
    down_grad = lax.dot_general(
        columns, grad_coarse, (((0,), (0,)), ((), ())), preferred_element_type=jnp.float32
    )
    grad_pre = (grad_hidden.astype(jnp.float32) * silu_slope(pre_act) * occupancy[:, None]).astype(
        jnp.bfloat16
    )
    padded_g = pad_bricks(
        halo_table(grad_pre.reshape(bricks, voxels, channels), send_list), link_rows
    )
    grad_in = (conv_transpose(padded_g, w_sub) * occupancy[:, None]).astype(jnp.bfloat16)
    sub_grad = weight_grad(padded_x, grad_pre)
    inverse_count = 1.0 / (lax.axis_size("space") * lax.axis_size("rep"))
    flat = jnp.concatenate([sub_grad.reshape(-1), down_grad.reshape(-1)])
    flat = tree_psum(flat, reduce_steps())
    sub_total = flat[: sub_grad.size].reshape(sub_grad.shape)
    down_total = flat[sub_grad.size :].reshape(down_grad.shape)
    return (
        coarse.reshape(1, bricks, voxels // 8, out_channels),
        grad_in.reshape(1, bricks, voxels, channels),
        sub_total * inverse_count,
        (down_total * inverse_count).reshape(w_down.shape),
    )


def solution(mesh):
    in_specs = (
        P("rep", "space", None, None),
        P("rep", "space", None),
        P("rep", "space", None),
        P("rep", "space"),
        P(),
        P(),
        P("rep", "space", None, None),
    )
    out_specs = (P("rep", "space", None, None), P("rep", "space", None, None), P(), P())
    return jax.shard_map(body, mesh=mesh, in_specs=in_specs, out_specs=out_specs, check_vma=False)
```

```python
import jax
import numpy as np
import jax.numpy as jnp
from jax import lax
from jax.sharding import PartitionSpec as P


def from_behind(value, axis, steps):
    count = lax.axis_size(axis)
    leading, last = (max(0, -steps), min(count, count - steps))
    return lax.ppermute(value, axis, [(source, source + steps) for source in range(leading, last)])


def _xor_pairs(count, bit):
    return [(index, index ^ bit) for index in range(count)]


def tree_psum(flat, steps):
    buf = flat
    for axis, bit in steps:
        me = (lax.axis_index(axis) // bit) % 2
        halves = buf.reshape(2, -1)
        keep = lax.dynamic_index_in_dim(halves, me, 0, keepdims=False)
        send = lax.dynamic_index_in_dim(halves, 1 - me, 0, keepdims=False)
        buf = keep + lax.ppermute(send, axis, _xor_pairs(lax.axis_size(axis), bit))
    for axis, bit in reversed(steps):
        me = (lax.axis_index(axis) // bit) % 2
        pair = jnp.stack([buf, lax.ppermute(buf, axis, _xor_pairs(lax.axis_size(axis), bit))])
        first = lax.dynamic_index_in_dim(pair, me, 0, keepdims=False)
        second = lax.dynamic_index_in_dim(pair, 1 - me, 0, keepdims=False)
        buf = jnp.concatenate([first, second])
    return buf


def reduce_steps():
    steps = [("rep", bit) for bit in (1, 2, 4) if bit < lax.axis_size("rep")]
    count = lax.axis_size("space")
    preferred = [1, 4, 16, 2, 8, 32, 64]
    bits = [bit for bit in preferred if bit < count]
    bits += [1 << k for k in range(count.bit_length()) if (1 << k) < count and (1 << k) not in bits]
    return steps + [("space", bit) for bit in bits]


def padding_maps():
    side = np.array([0] + [1] * 8 + [2])
    inner = (np.arange(10) - 1) % 8
    column = side[:, None, None] * 9 + side[None, :, None] * 3 + side[None, None, :]
    voxel = inner[:, None, None] * 64 + inner[None, :, None] * 8 + inner[None, None, :]
    return column, voxel


def halo_table(values, send_list):
    bricks, voxels, channels = values.shape
    cells = send_list.shape[0]
    slot_row = jnp.zeros((1, channels), values.dtype).at[0, :cells].set(send_list.astype(values.dtype))
    payload = jnp.concatenate([values.reshape(bricks * voxels, channels), slot_row], axis=0)
    from_lower = from_behind(payload, "space", 1)
    from_upper = from_behind(payload, "space", -1)
    table = jnp.concatenate(
        [
            values.reshape(bricks * voxels, channels),
            from_lower[: bricks * voxels],
            from_upper[: bricks * voxels],
            jnp.zeros((voxels, channels), values.dtype),
        ],
        axis=0,
    )
    lower_slots = from_lower[bricks * voxels, :cells].astype(jnp.int32)
    upper_slots = from_upper[bricks * voxels, :cells].astype(jnp.int32)
    return table, lower_slots, upper_slots


def brick_rows(link_rows, lower_slots, upper_slots, bricks):
    cells = lower_slots.shape[0]
    empty = 3 * bricks
    lower = jnp.take(lower_slots, jnp.clip(link_rows - bricks, 0, cells - 1), mode="clip")
    upper = jnp.take(upper_slots, jnp.clip(link_rows - bricks - cells, 0, cells - 1), mode="clip")
    lower = jnp.where(lower < bricks, bricks + lower, empty)
    upper = jnp.where(upper < bricks, 2 * bricks + upper, empty)
    from_upper = jnp.where(link_rows < bricks + 2 * cells, upper, empty)
    from_side = jnp.where(link_rows < bricks + cells, lower, from_upper)
    return jnp.where(link_rows < bricks, link_rows, from_side)


def pad_bricks(table, rows, voxels):
    column, voxel = padding_maps()
    index = jnp.take(rows, jnp.asarray(column.reshape(-1)), axis=1, mode="clip") * voxels
    index = index + jnp.asarray(voxel.reshape(1, -1))
    padded = jnp.take(table, index.reshape(-1), axis=0, mode="clip")
    return padded.reshape(rows.shape[0], 10, 10, 10, table.shape[-1])


DIMS = ("NDHWC", "DHWIO", "NDHWC")


def conv_forward(padded, w_sub):
    channels = w_sub.shape[1]
    kernel = w_sub.reshape(3, 3, 3, channels, w_sub.shape[2])
    out = lax.conv_general_dilated(
        padded, kernel, (1, 1, 1), "VALID", dimension_numbers=DIMS,
        preferred_element_type=jnp.float32,
    )
    return out.reshape(-1, w_sub.shape[2])


def conv_transpose(padded, w_sub):
    kernel = w_sub.reshape(3, 3, 3, w_sub.shape[1], w_sub.shape[2])[::-1, ::-1, ::-1]
    kernel = kernel.transpose(0, 1, 2, 4, 3)
    out = lax.conv_general_dilated(
        padded, kernel, (1, 1, 1), "VALID", dimension_numbers=DIMS,
        preferred_element_type=jnp.float32,
    )
    return out.reshape(-1, w_sub.shape[1])


def weight_grad(padded, grad_rows):
    bricks = padded.shape[0]
    channels = padded.shape[-1]
    grads = grad_rows.reshape(bricks, 8, 8, 8, grad_rows.shape[-1])
    numbers = lax.ConvDimensionNumbers(
        lhs_spec=(4, 0, 1, 2, 3), rhs_spec=(4, 0, 1, 2, 3), out_spec=(3, 4, 0, 1, 2)
    )
    out = lax.conv_general_dilated(
        padded, grads, (1, 1, 1), "VALID", dimension_numbers=numbers,
        preferred_element_type=jnp.float32,
    )
    return out.reshape(27, channels, grad_rows.shape[-1])


def to_columns(values):
    bricks = values.shape[0]
    channels = values.shape[-1]
    cube = values.reshape(bricks, 4, 2, 4, 2, 4, 2, channels)
    return cube.transpose(0, 1, 3, 5, 2, 4, 6, 7).reshape(bricks * 64, 8 * channels)


def from_columns(columns, bricks, channels):
    cube = columns.reshape(bricks, 4, 4, 4, 2, 2, 2, channels)
    return cube.transpose(0, 1, 4, 2, 5, 3, 6, 7).reshape(bricks, 512, channels)


def silu_slope(values):
    sigmoid_value = jax.nn.sigmoid(values)
    return sigmoid_value * (1.0 + values * (1.0 - sigmoid_value))


def body(features, voxel_mask, neighbours, send_slots, w_sub, w_down, cotangent):
    values = features[0]
    bricks, voxels, channels = values.shape
    out_channels = w_down.shape[2]
    link_rows = neighbours[0]
    send_list = send_slots[0]
    occupancy = voxel_mask[0].reshape(-1).astype(jnp.float32)
    masked = values * voxel_mask[0][..., None].astype(jnp.bfloat16)
    table_x, lower_slots, upper_slots = halo_table(masked, send_list)
    rows = brick_rows(link_rows, lower_slots, upper_slots, bricks)
    padded_x = pad_bricks(table_x, rows, voxels)
    pre_act = conv_forward(padded_x, w_sub) * occupancy[:, None]
    hidden = jax.nn.silu(pre_act).astype(jnp.bfloat16)
    columns = to_columns(hidden.reshape(bricks, voxels, channels))
    down_flat = w_down.reshape(-1, out_channels)
    coarse_mask = jnp.max(to_columns(occupancy.reshape(bricks, voxels, 1)), axis=1)
    coarse = (
        jnp.dot(columns, down_flat, preferred_element_type=jnp.float32) * coarse_mask[:, None]
    ).astype(jnp.bfloat16)
    grad_coarse = cotangent[0].reshape(-1, out_channels) * coarse_mask[:, None].astype(jnp.bfloat16)
    grad_cols = jnp.dot(grad_coarse, down_flat.T, preferred_element_type=jnp.float32).astype(
        jnp.bfloat16
    )
    grad_hidden = from_columns(grad_cols, bricks, channels).reshape(-1, channels)
    down_grad = lax.dot_general(
        columns, grad_coarse, (((0,), (0,)), ((), ())), preferred_element_type=jnp.float32
    )
    grad_pre = (grad_hidden.astype(jnp.float32) * silu_slope(pre_act) * occupancy[:, None]).astype(
        jnp.bfloat16
    )
    table_g, _, _ = halo_table(grad_pre.reshape(bricks, voxels, channels), send_list)
    padded_g = pad_bricks(table_g, rows, voxels)
    grad_in = (conv_transpose(padded_g, w_sub) * occupancy[:, None]).astype(jnp.bfloat16)
    sub_grad = weight_grad(padded_x, grad_pre)
    inverse_count = 1.0 / (lax.axis_size("space") * lax.axis_size("rep"))
    flat = jnp.concatenate([sub_grad.reshape(-1), down_grad.reshape(-1)])
    flat = tree_psum(flat, reduce_steps())
    sub_total = flat[: sub_grad.size].reshape(sub_grad.shape)
    down_total = flat[sub_grad.size :].reshape(down_grad.shape)
    return (
        coarse.reshape(1, bricks, voxels // 8, out_channels),
        grad_in.reshape(1, bricks, voxels, channels),
        sub_total * inverse_count,
        (down_total * inverse_count).reshape(w_down.shape),
    )


def solution(mesh):
    in_specs = (
        P("rep", "space", None, None),
        P("rep", "space", None),
        P("rep", "space", None),
        P("rep", "space"),
        P(),
        P(),
        P("rep", "space", None, None),
    )
    out_specs = (P("rep", "space", None, None), P("rep", "space", None, None), P(), P())
    return jax.shard_map(body, mesh=mesh, in_specs=in_specs, out_specs=out_specs, check_vma=False)
```

```python
import jax
import numpy as np
import jax.numpy as jnp
from jax import lax
from jax.sharding import PartitionSpec as P


def from_behind(value, axis, steps):
    count = lax.axis_size(axis)
    leading, last = (max(0, -steps), min(count, count - steps))
    return lax.ppermute(value, axis, [(source, source + steps) for source in range(leading, last)])


def _xor_pairs(count, mask):
    return [(index, index ^ mask) for index in range(count)]


def _member(axis, bits):
    index = lax.axis_index(axis)
    return sum(((index // bit) % 2) << k for k, bit in enumerate(bits))


def _mask(bits, step):
    return sum(bit for k, bit in enumerate(bits) if (step >> k) & 1)


def group_psum(flat, groups):
    buf = flat
    for axis, bits in groups:
        size = 1 << len(bits)
        count = lax.axis_size(axis)
        me = _member(axis, bits)
        chunks = buf.reshape(size, -1)
        total = lax.dynamic_index_in_dim(chunks, me, 0, keepdims=False)
        for step in range(1, size):
            send = lax.dynamic_index_in_dim(chunks, me ^ step, 0, keepdims=False)
            total = total + lax.ppermute(send, axis, _xor_pairs(count, _mask(bits, step)))
        buf = total
    for axis, bits in reversed(groups):
        size = 1 << len(bits)
        count = lax.axis_size(axis)
        me = _member(axis, bits)
        pieces = [buf] + [
            lax.ppermute(buf, axis, _xor_pairs(count, _mask(bits, step))) for step in range(1, size)
        ]
        order = jnp.arange(size, dtype=jnp.int32) ^ me
        buf = jnp.take(jnp.stack(pieces), order, axis=0, mode="clip").reshape(-1)
    return buf


def reduce_groups():
    groups = [("rep", [bit]) for bit in (1, 2, 4) if bit < lax.axis_size("rep")]
    count = lax.axis_size("space")
    if count == 128:
        return groups + [("space", [1, 2]), ("space", [4, 8]), ("space", [16, 32, 64])]
    return groups + [("space", [1 << k]) for k in range(count.bit_length() - 1)]


def padding_maps():
    side = np.array([0] + [1] * 8 + [2])
    inner = (np.arange(10) - 1) % 8
    column = side[:, None, None] * 9 + side[None, :, None] * 3 + side[None, None, :]
    voxel = inner[:, None, None] * 64 + inner[None, :, None] * 8 + inner[None, None, :]
    return column, voxel


def halo_table(values, send_list):
    bricks, voxels, channels = values.shape
    cells = send_list.shape[0]
    slot_row = jnp.zeros((1, channels), values.dtype).at[0, :cells].set(send_list.astype(values.dtype))
    payload = jnp.concatenate([values.reshape(bricks * voxels, channels), slot_row], axis=0)
    from_lower = from_behind(payload, "space", 1)
    from_upper = from_behind(payload, "space", -1)
    table = jnp.concatenate(
        [
            values.reshape(bricks * voxels, channels),
            from_lower[: bricks * voxels],
            from_upper[: bricks * voxels],
            jnp.zeros((voxels, channels), values.dtype),
        ],
        axis=0,
    )
    lower_slots = from_lower[bricks * voxels, :cells].astype(jnp.int32)
    upper_slots = from_upper[bricks * voxels, :cells].astype(jnp.int32)
    return table, lower_slots, upper_slots


def brick_rows(link_rows, lower_slots, upper_slots, bricks):
    cells = lower_slots.shape[0]
    empty = 3 * bricks
    lower = jnp.take(lower_slots, jnp.clip(link_rows - bricks, 0, cells - 1), mode="clip")
    upper = jnp.take(upper_slots, jnp.clip(link_rows - bricks - cells, 0, cells - 1), mode="clip")
    lower = jnp.where(lower < bricks, bricks + lower, empty)
    upper = jnp.where(upper < bricks, 2 * bricks + upper, empty)
    from_upper = jnp.where(link_rows < bricks + 2 * cells, upper, empty)
    from_side = jnp.where(link_rows < bricks + cells, lower, from_upper)
    return jnp.where(link_rows < bricks, link_rows, from_side)


def pad_bricks(table, rows, voxels):
    column, voxel = padding_maps()
    index = jnp.take(rows, jnp.asarray(column.reshape(-1)), axis=1, mode="clip") * voxels
    index = index + jnp.asarray(voxel.reshape(1, -1))
    padded = jnp.take(table, index.reshape(-1), axis=0, mode="clip")
    return padded.reshape(rows.shape[0], 10, 10, 10, table.shape[-1])


DIMS = ("NDHWC", "DHWIO", "NDHWC")


def conv_forward(padded, w_sub):
    channels = w_sub.shape[1]
    kernel = w_sub.reshape(3, 3, 3, channels, w_sub.shape[2])
    out = lax.conv_general_dilated(
        padded, kernel, (1, 1, 1), "VALID", dimension_numbers=DIMS,
        preferred_element_type=jnp.float32,
    )
    return out.reshape(-1, w_sub.shape[2])


def conv_transpose(padded, w_sub):
    kernel = w_sub.reshape(3, 3, 3, w_sub.shape[1], w_sub.shape[2])[::-1, ::-1, ::-1]
    kernel = kernel.transpose(0, 1, 2, 4, 3)
    out = lax.conv_general_dilated(
        padded, kernel, (1, 1, 1), "VALID", dimension_numbers=DIMS,
        preferred_element_type=jnp.float32,
    )
    return out.reshape(-1, w_sub.shape[1])


def weight_grad(padded, grad_rows):
    bricks = padded.shape[0]
    channels = padded.shape[-1]
    grads = grad_rows.reshape(bricks, 8, 8, 8, grad_rows.shape[-1])
    numbers = lax.ConvDimensionNumbers(
        lhs_spec=(4, 0, 1, 2, 3), rhs_spec=(4, 0, 1, 2, 3), out_spec=(3, 4, 0, 1, 2)
    )
    out = lax.conv_general_dilated(
        padded, grads, (1, 1, 1), "VALID", dimension_numbers=numbers,
        preferred_element_type=jnp.float32,
    )
    return out.reshape(27, channels, grad_rows.shape[-1])


def to_columns(values):
    bricks = values.shape[0]
    channels = values.shape[-1]
    cube = values.reshape(bricks, 4, 2, 4, 2, 4, 2, channels)
    return cube.transpose(0, 1, 3, 5, 2, 4, 6, 7).reshape(bricks * 64, 8 * channels)


def from_columns(columns, bricks, channels):
    cube = columns.reshape(bricks, 4, 4, 4, 2, 2, 2, channels)
    return cube.transpose(0, 1, 4, 2, 5, 3, 6, 7).reshape(bricks, 512, channels)


def silu_slope(values):
    sigmoid_value = jax.nn.sigmoid(values)
    return sigmoid_value * (1.0 + values * (1.0 - sigmoid_value))


def body(features, voxel_mask, neighbours, send_slots, w_sub, w_down, cotangent):
    values = features[0]
    bricks, voxels, channels = values.shape
    out_channels = w_down.shape[2]
    link_rows = neighbours[0]
    send_list = send_slots[0]
    occupancy = voxel_mask[0].reshape(-1).astype(jnp.float32)
    masked = values * voxel_mask[0][..., None].astype(jnp.bfloat16)
    table_x, lower_slots, upper_slots = halo_table(masked, send_list)
    rows = brick_rows(link_rows, lower_slots, upper_slots, bricks)
    padded_x = pad_bricks(table_x, rows, voxels)
    pre_act = conv_forward(padded_x, w_sub) * occupancy[:, None]
    hidden = jax.nn.silu(pre_act).astype(jnp.bfloat16)
    columns = to_columns(hidden.reshape(bricks, voxels, channels))
    down_flat = w_down.reshape(-1, out_channels)
    coarse_mask = jnp.max(to_columns(occupancy.reshape(bricks, voxels, 1)), axis=1)
    coarse = (
        jnp.dot(columns, down_flat, preferred_element_type=jnp.float32) * coarse_mask[:, None]
    ).astype(jnp.bfloat16)
    grad_coarse = cotangent[0].reshape(-1, out_channels) * coarse_mask[:, None].astype(jnp.bfloat16)
    grad_cols = jnp.dot(grad_coarse, down_flat.T, preferred_element_type=jnp.float32).astype(
        jnp.bfloat16
    )
    grad_hidden = from_columns(grad_cols, bricks, channels).reshape(-1, channels)
    down_grad = lax.dot_general(
        columns, grad_coarse, (((0,), (0,)), ((), ())), preferred_element_type=jnp.float32
    )
    grad_pre = (grad_hidden.astype(jnp.float32) * silu_slope(pre_act) * occupancy[:, None]).astype(
        jnp.bfloat16
    )
    table_g, _, _ = halo_table(grad_pre.reshape(bricks, voxels, channels), send_list)
    sub_grad, table_g = lax.optimization_barrier((weight_grad(padded_x, grad_pre), table_g))
    padded_g = pad_bricks(table_g, rows, voxels)
    grad_in = (conv_transpose(padded_g, w_sub) * occupancy[:, None]).astype(jnp.bfloat16)
    inverse_count = 1.0 / (lax.axis_size("space") * lax.axis_size("rep"))
    flat = jnp.concatenate([sub_grad.reshape(-1), down_grad.reshape(-1)])
    flat = group_psum(flat, reduce_groups())
    sub_total = flat[: sub_grad.size].reshape(sub_grad.shape)
    down_total = flat[sub_grad.size :].reshape(down_grad.shape)
    return (
        coarse.reshape(1, bricks, voxels // 8, out_channels),
        grad_in.reshape(1, bricks, voxels, channels),
        sub_total * inverse_count,
        (down_total * inverse_count).reshape(w_down.shape),
    )


def solution(mesh):
    in_specs = (
        P("rep", "space", None, None),
        P("rep", "space", None),
        P("rep", "space", None),
        P("rep", "space"),
        P(),
        P(),
        P("rep", "space", None, None),
    )
    out_specs = (P("rep", "space", None, None), P("rep", "space", None, None), P(), P())
    return jax.shard_map(body, mesh=mesh, in_specs=in_specs, out_specs=out_specs, check_vma=False)
```

```python
import jax
import numpy as np
import jax.numpy as jnp
from jax import lax
from jax.sharding import PartitionSpec as P


def from_behind(value, axis, steps):
    count = lax.axis_size(axis)
    leading, last = (max(0, -steps), min(count, count - steps))
    return lax.ppermute(value, axis, [(source, source + steps) for source in range(leading, last)])


HALVE = (None, (1, 4), (4, 16), (16, 1))
SPREAD = ((2, 8), (8, 32), (32, 64), (64, 2))


def joint_pairs(space_count, rep_count, masks):
    pairs = []
    for space in range(space_count):
        for rep in range(rep_count):
            if masks is None:
                target = space * rep_count + (rep ^ 1)
            else:
                target = (space ^ masks[rep]) * rep_count + rep
            pairs.append((space * rep_count + rep, target))
    return pairs


def step_bit(masks):
    rep = lax.axis_index("rep")
    if masks is None:
        return rep
    mask = jnp.where(rep == 0, masks[0], masks[1])
    return ((lax.axis_index("space") & mask) > 0).astype(jnp.int32)


def joint_psum(buf):
    axes = ("space", "rep")
    counts = (lax.axis_size("space"), lax.axis_size("rep"))
    for masks in HALVE:
        me = step_bit(masks)
        halves = buf.reshape(2, buf.shape[0] // 2, buf.shape[1])
        keep = lax.dynamic_index_in_dim(halves, me, 0, keepdims=False)
        send = lax.dynamic_index_in_dim(halves, 1 - me, 0, keepdims=False)
        buf = keep + lax.ppermute(send, axes, joint_pairs(*counts, masks))
    for masks in SPREAD:
        buf = buf + lax.ppermute(buf, axes, joint_pairs(*counts, masks))
    for masks in reversed(HALVE):
        me = step_bit(masks)
        other = lax.ppermute(buf, axes, joint_pairs(*counts, masks))
        buf = jnp.where(me == 0, jnp.concatenate([buf, other]), jnp.concatenate([other, buf]))
    return buf


def padding_maps():
    side = np.array([0] + [1] * 8 + [2])
    inner = (np.arange(10) - 1) % 8
    column = side[:, None, None] * 9 + side[None, :, None] * 3 + side[None, None, :]
    voxel = inner[:, None, None] * 64 + inner[None, :, None] * 8 + inner[None, None, :]
    return column, voxel


def halo_table(values, send_list):
    bricks, voxels, channels = values.shape
    cells = send_list.shape[0]
    slot_row = jnp.zeros((1, channels), values.dtype).at[0, :cells].set(send_list.astype(values.dtype))
    payload = jnp.concatenate([values.reshape(bricks * voxels, channels), slot_row], axis=0)
    from_lower = from_behind(payload, "space", 1)
    from_upper = from_behind(payload, "space", -1)
    table = jnp.concatenate(
        [
            values.reshape(bricks * voxels, channels),
            from_lower[: bricks * voxels],
            from_upper[: bricks * voxels],
            jnp.zeros((voxels, channels), values.dtype),
        ],
        axis=0,
    )
    lower_slots = from_lower[bricks * voxels, :cells].astype(jnp.int32)
    upper_slots = from_upper[bricks * voxels, :cells].astype(jnp.int32)
    return table, lower_slots, upper_slots


def brick_rows(link_rows, lower_slots, upper_slots, bricks):
    cells = lower_slots.shape[0]
    empty = 3 * bricks
    lower = jnp.take(lower_slots, jnp.clip(link_rows - bricks, 0, cells - 1), mode="clip")
    upper = jnp.take(upper_slots, jnp.clip(link_rows - bricks - cells, 0, cells - 1), mode="clip")
    lower = jnp.where(lower < bricks, bricks + lower, empty)
    upper = jnp.where(upper < bricks, 2 * bricks + upper, empty)
    from_upper = jnp.where(link_rows < bricks + 2 * cells, upper, empty)
    from_side = jnp.where(link_rows < bricks + cells, lower, from_upper)
    return jnp.where(link_rows < bricks, link_rows, from_side)


def pad_bricks(table, rows, voxels):
    column, voxel = padding_maps()
    index = jnp.take(rows, jnp.asarray(column.reshape(-1)), axis=1, mode="clip") * voxels
    index = index + jnp.asarray(voxel.reshape(1, -1))
    padded = jnp.take(table, index.reshape(-1), axis=0, mode="clip")
    return padded.reshape(rows.shape[0], 10, 10, 10, table.shape[-1])


DIMS = ("NDHWC", "DHWIO", "NDHWC")


def conv_forward(padded, w_sub):
    channels = w_sub.shape[1]
    kernel = w_sub.reshape(3, 3, 3, channels, w_sub.shape[2])
    out = lax.conv_general_dilated(
        padded, kernel, (1, 1, 1), "VALID", dimension_numbers=DIMS,
        preferred_element_type=jnp.float32,
    )
    return out.reshape(-1, w_sub.shape[2])


def conv_transpose(padded, w_sub):
    kernel = w_sub.reshape(3, 3, 3, w_sub.shape[1], w_sub.shape[2])[::-1, ::-1, ::-1]
    kernel = kernel.transpose(0, 1, 2, 4, 3)
    out = lax.conv_general_dilated(
        padded, kernel, (1, 1, 1), "VALID", dimension_numbers=DIMS,
        preferred_element_type=jnp.float32,
    )
    return out.reshape(-1, w_sub.shape[1])


def weight_grad(padded, grad_rows):
    bricks = padded.shape[0]
    channels = padded.shape[-1]
    grads = grad_rows.reshape(bricks, 8, 8, 8, grad_rows.shape[-1])
    numbers = lax.ConvDimensionNumbers(
        lhs_spec=(4, 0, 1, 2, 3), rhs_spec=(4, 0, 1, 2, 3), out_spec=(3, 4, 0, 1, 2)
    )
    out = lax.conv_general_dilated(
        padded, grads, (1, 1, 1), "VALID", dimension_numbers=numbers,
        preferred_element_type=jnp.float32,
    )
    return out.reshape(27, channels, grad_rows.shape[-1])


def to_columns(values):
    bricks = values.shape[0]
    channels = values.shape[-1]
    cube = values.reshape(bricks, 4, 2, 4, 2, 4, 2, channels)
    return cube.transpose(0, 1, 3, 5, 2, 4, 6, 7).reshape(bricks * 64, 8 * channels)


def from_columns(columns, bricks, channels):
    cube = columns.reshape(bricks, 4, 4, 4, 2, 2, 2, channels)
    return cube.transpose(0, 1, 4, 2, 5, 3, 6, 7).reshape(bricks, 512, channels)


def silu_slope(values):
    sigmoid_value = jax.nn.sigmoid(values)
    return sigmoid_value * (1.0 + values * (1.0 - sigmoid_value))


def body(features, voxel_mask, neighbours, send_slots, w_sub, w_down, cotangent):
    values = features[0]
    bricks, voxels, channels = values.shape
    out_channels = w_down.shape[2]
    link_rows = neighbours[0]
    send_list = send_slots[0]
    occupancy = voxel_mask[0].reshape(-1).astype(jnp.float32)
    masked = values * voxel_mask[0][..., None].astype(jnp.bfloat16)
    table_x, lower_slots, upper_slots = halo_table(masked, send_list)
    rows = brick_rows(link_rows, lower_slots, upper_slots, bricks)
    padded_x = pad_bricks(table_x, rows, voxels)
    pre_act = conv_forward(padded_x, w_sub) * occupancy[:, None]
    hidden = jax.nn.silu(pre_act).astype(jnp.bfloat16)
    columns = to_columns(hidden.reshape(bricks, voxels, channels))
    down_flat = w_down.reshape(-1, out_channels)
    coarse_mask = jnp.max(to_columns(occupancy.reshape(bricks, voxels, 1)), axis=1)
    coarse = (
        jnp.dot(columns, down_flat, preferred_element_type=jnp.float32) * coarse_mask[:, None]
    ).astype(jnp.bfloat16)
    grad_coarse = cotangent[0].reshape(-1, out_channels) * coarse_mask[:, None].astype(jnp.bfloat16)
    grad_cols = jnp.dot(grad_coarse, down_flat.T, preferred_element_type=jnp.float32).astype(
        jnp.bfloat16
    )
    grad_hidden = from_columns(grad_cols, bricks, channels).reshape(-1, channels)
    down_grad = lax.dot_general(
        columns, grad_coarse, (((0,), (0,)), ((), ())), preferred_element_type=jnp.float32
    )
    grad_pre = (grad_hidden.astype(jnp.float32) * silu_slope(pre_act) * occupancy[:, None]).astype(
        jnp.bfloat16
    )
    table_g, _, _ = halo_table(grad_pre.reshape(bricks, voxels, channels), send_list)
    sub_grad, table_g = lax.optimization_barrier((weight_grad(padded_x, grad_pre), table_g))
    padded_g = pad_bricks(table_g, rows, voxels)
    grad_in = (conv_transpose(padded_g, w_sub) * occupancy[:, None]).astype(jnp.bfloat16)
    inverse_count = 1.0 / (lax.axis_size("space") * lax.axis_size("rep"))
    lanes = 128
    flat = jnp.concatenate([sub_grad.reshape(-1, lanes), down_grad.reshape(-1, lanes)])
    flat = joint_psum(flat)
    split = sub_grad.size // lanes
    sub_total = flat[:split].reshape(sub_grad.shape)
    down_total = flat[split:].reshape(down_grad.shape)
    return (
        coarse.reshape(1, bricks, voxels // 8, out_channels),
        grad_in.reshape(1, bricks, voxels, channels),
        sub_total * inverse_count,
        (down_total * inverse_count).reshape(w_down.shape),
    )


def solution(mesh):
    in_specs = (
        P("rep", "space", None, None),
        P("rep", "space", None),
        P("rep", "space", None),
        P("rep", "space"),
        P(),
        P(),
        P("rep", "space", None, None),
    )
    out_specs = (P("rep", "space", None, None), P("rep", "space", None, None), P(), P())
    return jax.shard_map(body, mesh=mesh, in_specs=in_specs, out_specs=out_specs, check_vma=False)
```

```python
import jax
import numpy as np
import jax.numpy as jnp
from jax import lax
from jax.sharding import PartitionSpec as P


def from_behind(value, axis, steps):
    count = lax.axis_size(axis)
    leading, last = (max(0, -steps), min(count, count - steps))
    return lax.ppermute(value, axis, [(source, source + steps) for source in range(leading, last)])


HALVE = (None, (1, 4), (4, 16), (16, 1))
SPREAD = ((2, 8), (8, 32), (32, 64), (64, 2))


def joint_pairs(space_count, rep_count, masks):
    pairs = []
    for space in range(space_count):
        for rep in range(rep_count):
            if masks is None:
                target = space * rep_count + (rep ^ 1)
            else:
                target = (space ^ masks[rep]) * rep_count + rep
            pairs.append((space * rep_count + rep, target))
    return pairs


def step_bit(masks):
    rep = lax.axis_index("rep")
    if masks is None:
        return rep
    mask = jnp.where(rep == 0, masks[0], masks[1])
    return ((lax.axis_index("space") & mask) > 0).astype(jnp.int32)


def joint_psum(buf):
    axes = ("space", "rep")
    counts = (lax.axis_size("space"), lax.axis_size("rep"))
    wide = buf.dtype
    for masks in HALVE:
        me = step_bit(masks)
        halves = buf.reshape(2, buf.shape[0] // 2, buf.shape[1])
        keep = lax.dynamic_index_in_dim(halves, me, 0, keepdims=False)
        send = lax.dynamic_index_in_dim(halves, 1 - me, 0, keepdims=False).astype(jnp.bfloat16)
        buf = keep + lax.ppermute(send, axes, joint_pairs(*counts, masks)).astype(wide)
    for masks in SPREAD:
        narrow = buf.astype(jnp.bfloat16)
        other = lax.ppermute(narrow, axes, joint_pairs(*counts, masks))
        buf = narrow.astype(wide) + other.astype(wide)
    buf = buf.astype(jnp.bfloat16)
    for masks in reversed(HALVE):
        me = step_bit(masks)
        other = lax.ppermute(buf, axes, joint_pairs(*counts, masks))
        buf = jnp.where(me == 0, jnp.concatenate([buf, other]), jnp.concatenate([other, buf]))
    return buf.astype(wide)


def padding_maps():
    side = np.array([0] + [1] * 8 + [2])
    inner = (np.arange(10) - 1) % 8
    column = side[:, None, None] * 9 + side[None, :, None] * 3 + side[None, None, :]
    voxel = inner[:, None, None] * 64 + inner[None, :, None] * 8 + inner[None, None, :]
    return column, voxel


def halo_table(values, send_list):
    bricks, voxels, channels = values.shape
    cells = send_list.shape[0]
    slot_row = jnp.zeros((1, channels), values.dtype).at[0, :cells].set(send_list.astype(values.dtype))
    payload = jnp.concatenate([values.reshape(bricks * voxels, channels), slot_row], axis=0)
    from_lower = from_behind(payload, "space", 1)
    from_upper = from_behind(payload, "space", -1)
    table = jnp.concatenate(
        [
            values.reshape(bricks * voxels, channels),
            from_lower[: bricks * voxels],
            from_upper[: bricks * voxels],
            jnp.zeros((voxels, channels), values.dtype),
        ],
        axis=0,
    )
    lower_slots = from_lower[bricks * voxels, :cells].astype(jnp.int32)
    upper_slots = from_upper[bricks * voxels, :cells].astype(jnp.int32)
    return table, lower_slots, upper_slots


def brick_rows(link_rows, lower_slots, upper_slots, bricks):
    cells = lower_slots.shape[0]
    empty = 3 * bricks
    lower = jnp.take(lower_slots, jnp.clip(link_rows - bricks, 0, cells - 1), mode="clip")
    upper = jnp.take(upper_slots, jnp.clip(link_rows - bricks - cells, 0, cells - 1), mode="clip")
    lower = jnp.where(lower < bricks, bricks + lower, empty)
    upper = jnp.where(upper < bricks, 2 * bricks + upper, empty)
    from_upper = jnp.where(link_rows < bricks + 2 * cells, upper, empty)
    from_side = jnp.where(link_rows < bricks + cells, lower, from_upper)
    return jnp.where(link_rows < bricks, link_rows, from_side)


def pad_bricks(table, rows, voxels):
    column, voxel = padding_maps()
    index = jnp.take(rows, jnp.asarray(column.reshape(-1)), axis=1, mode="clip") * voxels
    index = index + jnp.asarray(voxel.reshape(1, -1))
    padded = jnp.take(table, index.reshape(-1), axis=0, mode="clip")
    return padded.reshape(rows.shape[0], 10, 10, 10, table.shape[-1])


DIMS = ("NDHWC", "DHWIO", "NDHWC")


def conv_forward(padded, w_sub):
    channels = w_sub.shape[1]
    kernel = w_sub.reshape(3, 3, 3, channels, w_sub.shape[2])
    out = lax.conv_general_dilated(
        padded, kernel, (1, 1, 1), "VALID", dimension_numbers=DIMS,
        preferred_element_type=jnp.float32,
    )
    return out.reshape(-1, w_sub.shape[2])


def conv_transpose(padded, w_sub):
    kernel = w_sub.reshape(3, 3, 3, w_sub.shape[1], w_sub.shape[2])[::-1, ::-1, ::-1]
    kernel = kernel.transpose(0, 1, 2, 4, 3)
    out = lax.conv_general_dilated(
        padded, kernel, (1, 1, 1), "VALID", dimension_numbers=DIMS,
        preferred_element_type=jnp.float32,
    )
    return out.reshape(-1, w_sub.shape[1])


def weight_grad(padded, grad_rows):
    bricks = padded.shape[0]
    channels = padded.shape[-1]
    grads = grad_rows.reshape(bricks, 8, 8, 8, grad_rows.shape[-1])
    numbers = lax.ConvDimensionNumbers(
        lhs_spec=(4, 0, 1, 2, 3), rhs_spec=(4, 0, 1, 2, 3), out_spec=(3, 4, 0, 1, 2)
    )
    out = lax.conv_general_dilated(
        padded, grads, (1, 1, 1), "VALID", dimension_numbers=numbers,
        preferred_element_type=jnp.float32,
    )
    return out.reshape(27, channels, grad_rows.shape[-1])


def to_columns(values):
    bricks = values.shape[0]
    channels = values.shape[-1]
    cube = values.reshape(bricks, 4, 2, 4, 2, 4, 2, channels)
    return cube.transpose(0, 1, 3, 5, 2, 4, 6, 7).reshape(bricks * 64, 8 * channels)


def from_columns(columns, bricks, channels):
    cube = columns.reshape(bricks, 4, 4, 4, 2, 2, 2, channels)
    return cube.transpose(0, 1, 4, 2, 5, 3, 6, 7).reshape(bricks, 512, channels)


def silu_slope(values):
    sigmoid_value = jax.nn.sigmoid(values)
    return sigmoid_value * (1.0 + values * (1.0 - sigmoid_value))


def body(features, voxel_mask, neighbours, send_slots, w_sub, w_down, cotangent):
    values = features[0]
    bricks, voxels, channels = values.shape
    out_channels = w_down.shape[2]
    link_rows = neighbours[0]
    send_list = send_slots[0]
    occupancy = voxel_mask[0].reshape(-1).astype(jnp.float32)
    masked = values * voxel_mask[0][..., None].astype(jnp.bfloat16)
    table_x, lower_slots, upper_slots = halo_table(masked, send_list)
    rows = brick_rows(link_rows, lower_slots, upper_slots, bricks)
    padded_x = pad_bricks(table_x, rows, voxels)
    pre_act = conv_forward(padded_x, w_sub) * occupancy[:, None]
    hidden = jax.nn.silu(pre_act).astype(jnp.bfloat16)
    columns = to_columns(hidden.reshape(bricks, voxels, channels))
    down_flat = w_down.reshape(-1, out_channels)
    coarse_mask = jnp.max(to_columns(occupancy.reshape(bricks, voxels, 1)), axis=1)
    coarse = (
        jnp.dot(columns, down_flat, preferred_element_type=jnp.float32) * coarse_mask[:, None]
    ).astype(jnp.bfloat16)
    grad_coarse = cotangent[0].reshape(-1, out_channels) * coarse_mask[:, None].astype(jnp.bfloat16)
    grad_cols = jnp.dot(grad_coarse, down_flat.T, preferred_element_type=jnp.float32).astype(
        jnp.bfloat16
    )
    grad_hidden = from_columns(grad_cols, bricks, channels).reshape(-1, channels)
    down_grad = lax.dot_general(
        columns, grad_coarse, (((0,), (0,)), ((), ())), preferred_element_type=jnp.float32
    )
    grad_pre = (grad_hidden.astype(jnp.float32) * silu_slope(pre_act) * occupancy[:, None]).astype(
        jnp.bfloat16
    )
    table_g, _, _ = halo_table(grad_pre.reshape(bricks, voxels, channels), send_list)
    sub_grad, table_g = lax.optimization_barrier((weight_grad(padded_x, grad_pre), table_g))
    padded_g = pad_bricks(table_g, rows, voxels)
    grad_in = (conv_transpose(padded_g, w_sub) * occupancy[:, None]).astype(jnp.bfloat16)
    inverse_count = 1.0 / (lax.axis_size("space") * lax.axis_size("rep"))
    lanes = 128
    flat = jnp.concatenate([sub_grad.reshape(-1, lanes), down_grad.reshape(-1, lanes)])
    flat = joint_psum(flat)
    split = sub_grad.size // lanes
    sub_total = flat[:split].reshape(sub_grad.shape)
    down_total = flat[split:].reshape(down_grad.shape)
    return (
        coarse.reshape(1, bricks, voxels // 8, out_channels),
        grad_in.reshape(1, bricks, voxels, channels),
        sub_total * inverse_count,
        (down_total * inverse_count).reshape(w_down.shape),
    )


def solution(mesh):
    in_specs = (
        P("rep", "space", None, None),
        P("rep", "space", None),
        P("rep", "space", None),
        P("rep", "space"),
        P(),
        P(),
        P("rep", "space", None, None),
    )
    out_specs = (P("rep", "space", None, None), P("rep", "space", None, None), P(), P())
    return jax.shard_map(body, mesh=mesh, in_specs=in_specs, out_specs=out_specs, check_vma=False)
```

```python
import jax
import numpy as np
import jax.numpy as jnp
from jax import lax
from jax.sharding import PartitionSpec as P


def from_behind(value, axis, steps):
    count = lax.axis_size(axis)
    leading, last = (max(0, -steps), min(count, count - steps))
    return lax.ppermute(value, axis, [(source, source + steps) for source in range(leading, last)])


HALVE = (None, (1, 4), (4, 16), (16, 1))
SPREAD = ((2, 8), (8, 32), (32, 64), (64, 2))


def joint_pairs(space_count, rep_count, masks):
    pairs = []
    for space in range(space_count):
        for rep in range(rep_count):
            if masks is None:
                target = space * rep_count + (rep ^ 1)
            else:
                target = (space ^ masks[rep]) * rep_count + rep
            pairs.append((space * rep_count + rep, target))
    return pairs


def step_bit(masks):
    rep = lax.axis_index("rep")
    if masks is None:
        return rep
    mask = jnp.where(rep == 0, masks[0], masks[1])
    return ((lax.axis_index("space") & mask) > 0).astype(jnp.int32)


def joint_psum(buf):
    axes = ("space", "rep")
    counts = (lax.axis_size("space"), lax.axis_size("rep"))
    wide = buf.dtype
    for masks in HALVE:
        me = step_bit(masks)
        halves = buf.reshape(2, buf.shape[0] // 2, buf.shape[1])
        keep = lax.dynamic_index_in_dim(halves, me, 0, keepdims=False)
        send = lax.dynamic_index_in_dim(halves, 1 - me, 0, keepdims=False).astype(jnp.bfloat16)
        buf = keep + lax.ppermute(send, axes, joint_pairs(*counts, masks)).astype(wide)
    for masks in SPREAD:
        narrow = buf.astype(jnp.bfloat16)
        other = lax.ppermute(narrow, axes, joint_pairs(*counts, masks))
        buf = narrow.astype(wide) + other.astype(wide)
    buf = buf.astype(jnp.bfloat16)
    for masks in reversed(HALVE):
        me = step_bit(masks)
        other = lax.ppermute(buf, axes, joint_pairs(*counts, masks))
        buf = jnp.where(me == 0, jnp.concatenate([buf, other]), jnp.concatenate([other, buf]))
    return buf.astype(wide)


def padding_maps():
    side = np.array([0] + [1] * 8 + [2])
    inner = (np.arange(10) - 1) % 8
    column = side[:, None, None] * 9 + side[None, :, None] * 3 + side[None, None, :]
    voxel = inner[:, None, None] * 64 + inner[None, :, None] * 8 + inner[None, None, :]
    return column, voxel


def halo_exchange(values, send_list):
    bricks, voxels, channels = values.shape
    cells = send_list.shape[0]
    slot_row = jnp.zeros((1, channels), values.dtype).at[0, :cells].set(send_list.astype(values.dtype))
    payload = jnp.concatenate([values.reshape(bricks * voxels, channels), slot_row], axis=0)
    return from_behind(payload, "space", 1), from_behind(payload, "space", -1)


def halo_table(values, received, cells):
    bricks, voxels, channels = values.shape
    from_lower, from_upper = received
    table = jnp.concatenate(
        [
            values.reshape(bricks * voxels, channels),
            from_lower[: bricks * voxels],
            from_upper[: bricks * voxels],
            jnp.zeros((voxels, channels), values.dtype),
        ],
        axis=0,
    )
    lower_slots = from_lower[bricks * voxels, :cells].astype(jnp.int32)
    upper_slots = from_upper[bricks * voxels, :cells].astype(jnp.int32)
    return table, lower_slots, upper_slots


def brick_rows(link_rows, lower_slots, upper_slots, bricks):
    cells = lower_slots.shape[0]
    empty = 3 * bricks
    lower = jnp.take(lower_slots, jnp.clip(link_rows - bricks, 0, cells - 1), mode="clip")
    upper = jnp.take(upper_slots, jnp.clip(link_rows - bricks - cells, 0, cells - 1), mode="clip")
    lower = jnp.where(lower < bricks, bricks + lower, empty)
    upper = jnp.where(upper < bricks, 2 * bricks + upper, empty)
    from_upper = jnp.where(link_rows < bricks + 2 * cells, upper, empty)
    from_side = jnp.where(link_rows < bricks + cells, lower, from_upper)
    return jnp.where(link_rows < bricks, link_rows, from_side)


def pad_bricks(table, rows, voxels):
    column, voxel = padding_maps()
    index = jnp.take(rows, jnp.asarray(column.reshape(-1)), axis=1, mode="clip") * voxels
    index = index + jnp.asarray(voxel.reshape(1, -1))
    padded = jnp.take(table, index.reshape(-1), axis=0, mode="clip")
    return padded.reshape(rows.shape[0], 10, 10, 10, table.shape[-1])


DIMS = ("NDHWC", "DHWIO", "NDHWC")


def conv_forward(padded, w_sub):
    channels = w_sub.shape[1]
    kernel = w_sub.reshape(3, 3, 3, channels, w_sub.shape[2])
    out = lax.conv_general_dilated(
        padded, kernel, (1, 1, 1), "VALID", dimension_numbers=DIMS,
        preferred_element_type=jnp.float32,
    )
    return out.reshape(-1, w_sub.shape[2])


def conv_transpose(padded, w_sub):
    kernel = w_sub.reshape(3, 3, 3, w_sub.shape[1], w_sub.shape[2])[::-1, ::-1, ::-1]
    kernel = kernel.transpose(0, 1, 2, 4, 3)
    out = lax.conv_general_dilated(
        padded, kernel, (1, 1, 1), "VALID", dimension_numbers=DIMS,
        preferred_element_type=jnp.float32,
    )
    return out.reshape(-1, w_sub.shape[1])


def weight_grad(padded, grad_rows):
    bricks = padded.shape[0]
    channels = padded.shape[-1]
    grads = grad_rows.reshape(bricks, 8, 8, 8, grad_rows.shape[-1])
    numbers = lax.ConvDimensionNumbers(
        lhs_spec=(4, 0, 1, 2, 3), rhs_spec=(4, 0, 1, 2, 3), out_spec=(3, 4, 0, 1, 2)
    )
    out = lax.conv_general_dilated(
        padded, grads, (1, 1, 1), "VALID", dimension_numbers=numbers,
        preferred_element_type=jnp.float32,
    )
    return out.reshape(27, channels, grad_rows.shape[-1])


def to_columns(values):
    bricks = values.shape[0]
    channels = values.shape[-1]
    cube = values.reshape(bricks, 4, 2, 4, 2, 4, 2, channels)
    return cube.transpose(0, 1, 3, 5, 2, 4, 6, 7).reshape(bricks * 64, 8 * channels)


def from_columns(columns, bricks, channels):
    cube = columns.reshape(bricks, 4, 4, 4, 2, 2, 2, channels)
    return cube.transpose(0, 1, 4, 2, 5, 3, 6, 7).reshape(bricks, 512, channels)


def silu_slope(values):
    sigmoid_value = jax.nn.sigmoid(values)
    return sigmoid_value * (1.0 + values * (1.0 - sigmoid_value))


def body(features, voxel_mask, neighbours, send_slots, w_sub, w_down, cotangent):
    values = features[0]
    bricks, voxels, channels = values.shape
    out_channels = w_down.shape[2]
    link_rows = neighbours[0]
    send_list = send_slots[0]
    occupancy = voxel_mask[0].reshape(-1).astype(jnp.float32)
    masked = values * voxel_mask[0][..., None].astype(jnp.bfloat16)
    cells = send_list.shape[0]
    table_x, lower_slots, upper_slots = halo_table(masked, halo_exchange(masked, send_list), cells)
    rows = brick_rows(link_rows, lower_slots, upper_slots, bricks)
    padded_x = pad_bricks(table_x, rows, voxels)
    pre_act = conv_forward(padded_x, w_sub) * occupancy[:, None]
    hidden = jax.nn.silu(pre_act).astype(jnp.bfloat16)
    columns = to_columns(hidden.reshape(bricks, voxels, channels))
    down_flat = w_down.reshape(-1, out_channels)
    coarse_mask = jnp.max(to_columns(occupancy.reshape(bricks, voxels, 1)), axis=1)
    coarse = (
        jnp.dot(columns, down_flat, preferred_element_type=jnp.float32) * coarse_mask[:, None]
    ).astype(jnp.bfloat16)
    grad_coarse = cotangent[0].reshape(-1, out_channels) * coarse_mask[:, None].astype(jnp.bfloat16)
    grad_cols = jnp.dot(grad_coarse, down_flat.T, preferred_element_type=jnp.float32).astype(
        jnp.bfloat16
    )
    grad_hidden = from_columns(grad_cols, bricks, channels).reshape(-1, channels)
    down_grad = lax.dot_general(
        columns, grad_coarse, (((0,), (0,)), ((), ())), preferred_element_type=jnp.float32
    )
    grad_pre = (grad_hidden.astype(jnp.float32) * silu_slope(pre_act) * occupancy[:, None]).astype(
        jnp.bfloat16
    )
    grad_pre_bricks = grad_pre.reshape(bricks, voxels, channels)
    received_g = halo_exchange(grad_pre_bricks, send_list)
    sub_grad, received_g = lax.optimization_barrier((weight_grad(padded_x, grad_pre), received_g))
    table_g, _, _ = halo_table(grad_pre_bricks, received_g, cells)
    padded_g = pad_bricks(table_g, rows, voxels)
    grad_in = (conv_transpose(padded_g, w_sub) * occupancy[:, None]).astype(jnp.bfloat16)
    inverse_count = 1.0 / (lax.axis_size("space") * lax.axis_size("rep"))
    lanes = 128
    flat = jnp.concatenate([sub_grad.reshape(-1, lanes), down_grad.reshape(-1, lanes)])
    flat = joint_psum(flat)
    split = sub_grad.size // lanes
    sub_total = flat[:split].reshape(sub_grad.shape)
    down_total = flat[split:].reshape(down_grad.shape)
    return (
        coarse.reshape(1, bricks, voxels // 8, out_channels),
        grad_in.reshape(1, bricks, voxels, channels),
        sub_total * inverse_count,
        (down_total * inverse_count).reshape(w_down.shape),
    )


def solution(mesh):
    in_specs = (
        P("rep", "space", None, None),
        P("rep", "space", None),
        P("rep", "space", None),
        P("rep", "space"),
        P(),
        P(),
        P("rep", "space", None, None),
    )
    out_specs = (P("rep", "space", None, None), P("rep", "space", None, None), P(), P())
    return jax.shard_map(body, mesh=mesh, in_specs=in_specs, out_specs=out_specs, check_vma=False)
```

```python
import jax
import numpy as np
import jax.numpy as jnp
from jax import lax
from jax.sharding import PartitionSpec as P


def from_behind(value, axis, steps):
    count = lax.axis_size(axis)
    leading, last = (max(0, -steps), min(count, count - steps))
    return lax.ppermute(value, axis, [(source, source + steps) for source in range(leading, last)])


HALVE = (None, (1, 4), (4, 16))
SPREAD = ((16, 1), (2, 8), (8, 32), (32, 64), (64, 2))


def joint_pairs(space_count, rep_count, masks):
    pairs = []
    for space in range(space_count):
        for rep in range(rep_count):
            if masks is None:
                target = space * rep_count + (rep ^ 1)
            else:
                target = (space ^ masks[rep]) * rep_count + rep
            pairs.append((space * rep_count + rep, target))
    return pairs


def step_bit(masks):
    rep = lax.axis_index("rep")
    if masks is None:
        return rep
    mask = jnp.where(rep == 0, masks[0], masks[1])
    return ((lax.axis_index("space") & mask) > 0).astype(jnp.int32)


def joint_psum(buf):
    axes = ("space", "rep")
    counts = (lax.axis_size("space"), lax.axis_size("rep"))
    wide = buf.dtype
    for masks in HALVE:
        me = step_bit(masks)
        halves = buf.reshape(2, buf.shape[0] // 2, buf.shape[1])
        keep = lax.dynamic_index_in_dim(halves, me, 0, keepdims=False)
        send = lax.dynamic_index_in_dim(halves, 1 - me, 0, keepdims=False).astype(jnp.bfloat16)
        buf = keep + lax.ppermute(send, axes, joint_pairs(*counts, masks)).astype(wide)
    for masks in SPREAD:
        narrow = buf.astype(jnp.bfloat16)
        other = lax.ppermute(narrow, axes, joint_pairs(*counts, masks))
        buf = narrow.astype(wide) + other.astype(wide)
    buf = buf.astype(jnp.bfloat16)
    for masks in reversed(HALVE):
        me = step_bit(masks)
        other = lax.ppermute(buf, axes, joint_pairs(*counts, masks))
        buf = jnp.where(me == 0, jnp.concatenate([buf, other]), jnp.concatenate([other, buf]))
    return buf.astype(wide)


def padding_maps():
    side = np.array([0] + [1] * 8 + [2])
    inner = (np.arange(10) - 1) % 8
    column = side[:, None, None] * 9 + side[None, :, None] * 3 + side[None, None, :]
    voxel = inner[:, None, None] * 64 + inner[None, :, None] * 8 + inner[None, None, :]
    return column, voxel


def halo_exchange(values, send_list):
    bricks, voxels, channels = values.shape
    cells = send_list.shape[0]
    slot_row = jnp.zeros((1, channels), values.dtype).at[0, :cells].set(send_list.astype(values.dtype))
    payload = jnp.concatenate([values.reshape(bricks * voxels, channels), slot_row], axis=0)
    return from_behind(payload, "space", 1), from_behind(payload, "space", -1)


def halo_table(values, received, cells):
    bricks, voxels, channels = values.shape
    from_lower, from_upper = received
    table = jnp.concatenate(
        [
            values.reshape(bricks * voxels, channels),
            from_lower[: bricks * voxels],
            from_upper[: bricks * voxels],
            jnp.zeros((voxels, channels), values.dtype),
        ],
        axis=0,
    )
    lower_slots = from_lower[bricks * voxels, :cells].astype(jnp.int32)
    upper_slots = from_upper[bricks * voxels, :cells].astype(jnp.int32)
    return table, lower_slots, upper_slots


def brick_rows(link_rows, lower_slots, upper_slots, bricks):
    cells = lower_slots.shape[0]
    empty = 3 * bricks
    lower = jnp.take(lower_slots, jnp.clip(link_rows - bricks, 0, cells - 1), mode="clip")
    upper = jnp.take(upper_slots, jnp.clip(link_rows - bricks - cells, 0, cells - 1), mode="clip")
    lower = jnp.where(lower < bricks, bricks + lower, empty)
    upper = jnp.where(upper < bricks, 2 * bricks + upper, empty)
    from_upper = jnp.where(link_rows < bricks + 2 * cells, upper, empty)
    from_side = jnp.where(link_rows < bricks + cells, lower, from_upper)
    return jnp.where(link_rows < bricks, link_rows, from_side)


def pad_bricks(table, rows, voxels):
    column, voxel = padding_maps()
    index = jnp.take(rows, jnp.asarray(column.reshape(-1)), axis=1, mode="clip") * voxels
    index = index + jnp.asarray(voxel.reshape(1, -1))
    padded = jnp.take(table, index.reshape(-1), axis=0, mode="clip")
    return padded.reshape(rows.shape[0], 10, 10, 10, table.shape[-1])


DIMS = ("NDHWC", "DHWIO", "NDHWC")


def conv_forward(padded, w_sub):
    channels = w_sub.shape[1]
    kernel = w_sub.reshape(3, 3, 3, channels, w_sub.shape[2])
    out = lax.conv_general_dilated(
        padded, kernel, (1, 1, 1), "VALID", dimension_numbers=DIMS,
        preferred_element_type=jnp.float32,
    )
    return out.reshape(-1, w_sub.shape[2])


def conv_transpose(padded, w_sub):
    kernel = w_sub.reshape(3, 3, 3, w_sub.shape[1], w_sub.shape[2])[::-1, ::-1, ::-1]
    kernel = kernel.transpose(0, 1, 2, 4, 3)
    out = lax.conv_general_dilated(
        padded, kernel, (1, 1, 1), "VALID", dimension_numbers=DIMS,
        preferred_element_type=jnp.float32,
    )
    return out.reshape(-1, w_sub.shape[1])


def weight_grad(padded, grad_rows):
    bricks = padded.shape[0]
    channels = padded.shape[-1]
    grads = grad_rows.reshape(bricks, 8, 8, 8, grad_rows.shape[-1])
    numbers = lax.ConvDimensionNumbers(
        lhs_spec=(4, 0, 1, 2, 3), rhs_spec=(4, 0, 1, 2, 3), out_spec=(3, 4, 0, 1, 2)
    )
    out = lax.conv_general_dilated(
        padded, grads, (1, 1, 1), "VALID", dimension_numbers=numbers,
        preferred_element_type=jnp.float32,
    )
    return out.reshape(27, channels, grad_rows.shape[-1])


def to_columns(values):
    bricks = values.shape[0]
    channels = values.shape[-1]
    cube = values.reshape(bricks, 4, 2, 4, 2, 4, 2, channels)
    return cube.transpose(0, 1, 3, 5, 2, 4, 6, 7).reshape(bricks * 64, 8 * channels)


def from_columns(columns, bricks, channels):
    cube = columns.reshape(bricks, 4, 4, 4, 2, 2, 2, channels)
    return cube.transpose(0, 1, 4, 2, 5, 3, 6, 7).reshape(bricks, 512, channels)


def silu_slope(values):
    sigmoid_value = jax.nn.sigmoid(values)
    return sigmoid_value * (1.0 + values * (1.0 - sigmoid_value))


def body(features, voxel_mask, neighbours, send_slots, w_sub, w_down, cotangent):
    values = features[0]
    bricks, voxels, channels = values.shape
    out_channels = w_down.shape[2]
    link_rows = neighbours[0]
    send_list = send_slots[0]
    occupancy = voxel_mask[0].reshape(-1).astype(jnp.float32)
    masked = values * voxel_mask[0][..., None].astype(jnp.bfloat16)
    cells = send_list.shape[0]
    table_x, lower_slots, upper_slots = halo_table(masked, halo_exchange(masked, send_list), cells)
    rows = brick_rows(link_rows, lower_slots, upper_slots, bricks)
    padded_x = pad_bricks(table_x, rows, voxels)
    pre_act = conv_forward(padded_x, w_sub) * occupancy[:, None]
    hidden = jax.nn.silu(pre_act).astype(jnp.bfloat16)
    columns = to_columns(hidden.reshape(bricks, voxels, channels))
    down_flat = w_down.reshape(-1, out_channels)
    coarse_mask = jnp.max(to_columns(occupancy.reshape(bricks, voxels, 1)), axis=1)
    coarse = (
        jnp.dot(columns, down_flat, preferred_element_type=jnp.float32) * coarse_mask[:, None]
    ).astype(jnp.bfloat16)
    grad_coarse = cotangent[0].reshape(-1, out_channels) * coarse_mask[:, None].astype(jnp.bfloat16)
    grad_cols = jnp.dot(grad_coarse, down_flat.T, preferred_element_type=jnp.float32).astype(
        jnp.bfloat16
    )
    grad_hidden = from_columns(grad_cols, bricks, channels).reshape(-1, channels)
    down_grad = lax.dot_general(
        columns, grad_coarse, (((0,), (0,)), ((), ())), preferred_element_type=jnp.float32
    )
    grad_pre = (grad_hidden.astype(jnp.float32) * silu_slope(pre_act) * occupancy[:, None]).astype(
        jnp.bfloat16
    )
    grad_pre_bricks = grad_pre.reshape(bricks, voxels, channels)
    received_g = halo_exchange(grad_pre_bricks, send_list)
    sub_grad, received_g = lax.optimization_barrier((weight_grad(padded_x, grad_pre), received_g))
    table_g, _, _ = halo_table(grad_pre_bricks, received_g, cells)
    padded_g = pad_bricks(table_g, rows, voxels)
    grad_in = (conv_transpose(padded_g, w_sub) * occupancy[:, None]).astype(jnp.bfloat16)
    inverse_count = 1.0 / (lax.axis_size("space") * lax.axis_size("rep"))
    lanes = 128
    flat = jnp.concatenate([sub_grad.reshape(-1, lanes), down_grad.reshape(-1, lanes)])
    flat = joint_psum(flat)
    split = sub_grad.size // lanes
    sub_total = flat[:split].reshape(sub_grad.shape)
    down_total = flat[split:].reshape(down_grad.shape)
    return (
        coarse.reshape(1, bricks, voxels // 8, out_channels),
        grad_in.reshape(1, bricks, voxels, channels),
        sub_total * inverse_count,
        (down_total * inverse_count).reshape(w_down.shape),
    )


def solution(mesh):
    in_specs = (
        P("rep", "space", None, None),
        P("rep", "space", None),
        P("rep", "space", None),
        P("rep", "space"),
        P(),
        P(),
        P("rep", "space", None, None),
    )
    out_specs = (P("rep", "space", None, None), P("rep", "space", None, None), P(), P())
    return jax.shard_map(body, mesh=mesh, in_specs=in_specs, out_specs=out_specs, check_vma=False)
```

```python
import jax
import numpy as np
import jax.numpy as jnp
from jax import lax
from jax.sharding import PartitionSpec as P


def from_behind(value, axis, steps):
    count = lax.axis_size(axis)
    leading, last = (max(0, -steps), min(count, count - steps))
    return lax.ppermute(value, axis, [(source, source + steps) for source in range(leading, last)])


HALVE = (None, (1, 4), (4, 16), (16, 1))
SPREAD = ((2, 8), (8, 32), (32, 64), (64, 2))


def joint_pairs(space_count, rep_count, masks):
    pairs = []
    for space in range(space_count):
        for rep in range(rep_count):
            if masks is None:
                target = space * rep_count + (rep ^ 1)
            else:
                target = (space ^ masks[rep]) * rep_count + rep
            pairs.append((space * rep_count + rep, target))
    return pairs


def step_bit(masks):
    rep = lax.axis_index("rep")
    if masks is None:
        return rep
    mask = jnp.where(rep == 0, masks[0], masks[1])
    return ((lax.axis_index("space") & mask) > 0).astype(jnp.int32)


def joint_psum(buf, scale):
    axes = ("space", "rep")
    counts = (lax.axis_size("space"), lax.axis_size("rep"))
    wide = buf.dtype
    for masks in HALVE:
        me = step_bit(masks)
        halves = buf.reshape(2, buf.shape[0] // 2, buf.shape[1])
        keep = lax.dynamic_index_in_dim(halves, me, 0, keepdims=False)
        send = lax.dynamic_index_in_dim(halves, 1 - me, 0, keepdims=False).astype(jnp.bfloat16)
        buf = keep + lax.ppermute(send, axes, joint_pairs(*counts, masks)).astype(wide)
    for masks in SPREAD:
        narrow = buf.astype(jnp.bfloat16)
        other = lax.ppermute(narrow, axes, joint_pairs(*counts, masks))
        buf = narrow.astype(wide) + other.astype(wide)
    buf = (buf * scale).astype(jnp.bfloat16)
    for masks in reversed(HALVE):
        me = step_bit(masks)
        other = lax.ppermute(buf, axes, joint_pairs(*counts, masks))
        buf = jnp.where(me == 0, jnp.concatenate([buf, other]), jnp.concatenate([other, buf]))
    return buf.astype(wide)


def padding_maps():
    side = np.array([0] + [1] * 8 + [2])
    inner = (np.arange(10) - 1) % 8
    column = side[:, None, None] * 9 + side[None, :, None] * 3 + side[None, None, :]
    voxel = inner[:, None, None] * 64 + inner[None, :, None] * 8 + inner[None, None, :]
    return column, voxel


def halo_exchange(values, send_list):
    bricks, voxels, channels = values.shape
    cells = send_list.shape[0]
    slot_row = jnp.zeros((1, channels), values.dtype).at[0, :cells].set(send_list.astype(values.dtype))
    payload = jnp.concatenate([values.reshape(bricks * voxels, channels), slot_row], axis=0)
    return from_behind(payload, "space", 1), from_behind(payload, "space", -1)


def halo_table(values, received, cells):
    bricks, voxels, channels = values.shape
    from_lower, from_upper = received
    table = jnp.concatenate(
        [
            values.reshape(bricks * voxels, channels),
            from_lower[: bricks * voxels],
            from_upper[: bricks * voxels],
            jnp.zeros((voxels, channels), values.dtype),
        ],
        axis=0,
    )
    lower_slots = from_lower[bricks * voxels, :cells].astype(jnp.int32)
    upper_slots = from_upper[bricks * voxels, :cells].astype(jnp.int32)
    return table, lower_slots, upper_slots


def brick_rows(link_rows, lower_slots, upper_slots, bricks):
    cells = lower_slots.shape[0]
    empty = 3 * bricks
    lower = jnp.take(lower_slots, jnp.clip(link_rows - bricks, 0, cells - 1), mode="clip")
    upper = jnp.take(upper_slots, jnp.clip(link_rows - bricks - cells, 0, cells - 1), mode="clip")
    lower = jnp.where(lower < bricks, bricks + lower, empty)
    upper = jnp.where(upper < bricks, 2 * bricks + upper, empty)
    from_upper = jnp.where(link_rows < bricks + 2 * cells, upper, empty)
    from_side = jnp.where(link_rows < bricks + cells, lower, from_upper)
    return jnp.where(link_rows < bricks, link_rows, from_side)


def pad_bricks(table, rows, voxels):
    column, voxel = padding_maps()
    picks = jnp.asarray(column.reshape(1, -1, 1) == np.arange(rows.shape[1]).reshape(1, 1, -1))
    index = jnp.sum(jnp.where(picks, rows[:, None, :], 0), axis=-1) * voxels
    index = index + jnp.asarray(voxel.reshape(1, -1))
    padded = jnp.take(table, index.reshape(-1), axis=0, mode="clip")
    return padded.reshape(rows.shape[0], 10, 10, 10, table.shape[-1])


DIMS = ("NDHWC", "DHWIO", "NDHWC")


def conv_forward(padded, w_sub):
    channels = w_sub.shape[1]
    kernel = w_sub.reshape(3, 3, 3, channels, w_sub.shape[2])
    out = lax.conv_general_dilated(
        padded, kernel, (1, 1, 1), "VALID", dimension_numbers=DIMS,
        preferred_element_type=jnp.float32,
    )
    return out.reshape(-1, w_sub.shape[2])


def conv_transpose(padded, w_sub):
    kernel = w_sub.reshape(3, 3, 3, w_sub.shape[1], w_sub.shape[2])[::-1, ::-1, ::-1]
    kernel = kernel.transpose(0, 1, 2, 4, 3)
    out = lax.conv_general_dilated(
        padded, kernel, (1, 1, 1), "VALID", dimension_numbers=DIMS,
        preferred_element_type=jnp.float32,
    )
    return out.reshape(-1, w_sub.shape[1])


def weight_grad(padded, grad_rows):
    bricks = padded.shape[0]
    channels = padded.shape[-1]
    grads = grad_rows.reshape(bricks, 8, 8, 8, grad_rows.shape[-1])
    numbers = lax.ConvDimensionNumbers(
        lhs_spec=(4, 0, 1, 2, 3), rhs_spec=(4, 0, 1, 2, 3), out_spec=(3, 4, 0, 1, 2)
    )
    out = lax.conv_general_dilated(
        padded, grads, (1, 1, 1), "VALID", dimension_numbers=numbers,
        preferred_element_type=jnp.float32,
    )
    return out.reshape(27, channels, grad_rows.shape[-1])


def to_columns(values):
    bricks = values.shape[0]
    channels = values.shape[-1]
    cube = values.reshape(bricks, 4, 2, 4, 2, 4, 2, channels)
    return cube.transpose(0, 1, 3, 5, 2, 4, 6, 7).reshape(bricks * 64, 8 * channels)


def from_columns(columns, bricks, channels):
    cube = columns.reshape(bricks, 4, 4, 4, 2, 2, 2, channels)
    return cube.transpose(0, 1, 4, 2, 5, 3, 6, 7).reshape(bricks, 512, channels)


def silu_slope(values):
    sigmoid_value = jax.nn.sigmoid(values)
    return sigmoid_value * (1.0 + values * (1.0 - sigmoid_value))


def body(features, voxel_mask, neighbours, send_slots, w_sub, w_down, cotangent):
    values = features[0]
    bricks, voxels, channels = values.shape
    out_channels = w_down.shape[2]
    link_rows = neighbours[0]
    send_list = send_slots[0]
    occupancy = voxel_mask[0].reshape(-1).astype(jnp.float32)
    masked = values * voxel_mask[0][..., None].astype(jnp.bfloat16)
    cells = send_list.shape[0]
    table_x, lower_slots, upper_slots = halo_table(masked, halo_exchange(masked, send_list), cells)
    rows = brick_rows(link_rows, lower_slots, upper_slots, bricks)
    padded_x = pad_bricks(table_x, rows, voxels)
    pre_act = conv_forward(padded_x, w_sub) * occupancy[:, None]
    hidden = jax.nn.silu(pre_act).astype(jnp.bfloat16)
    columns = to_columns(hidden.reshape(bricks, voxels, channels))
    down_flat = w_down.reshape(-1, out_channels)
    coarse_mask = jnp.max(to_columns(occupancy.reshape(bricks, voxels, 1)), axis=1)
    coarse = (
        jnp.dot(columns, down_flat, preferred_element_type=jnp.float32) * coarse_mask[:, None]
    ).astype(jnp.bfloat16)
    grad_coarse = cotangent[0].reshape(-1, out_channels) * coarse_mask[:, None].astype(jnp.bfloat16)
    grad_cols = jnp.dot(grad_coarse, down_flat.T, preferred_element_type=jnp.float32).astype(
        jnp.bfloat16
    )
    grad_hidden = from_columns(grad_cols, bricks, channels).reshape(-1, channels)
    down_grad = lax.dot_general(
        columns, grad_coarse, (((0,), (0,)), ((), ())), preferred_element_type=jnp.float32
    )
    grad_pre = (grad_hidden.astype(jnp.float32) * silu_slope(pre_act) * occupancy[:, None]).astype(
        jnp.bfloat16
    )
    grad_pre_bricks = grad_pre.reshape(bricks, voxels, channels)
    received_g = halo_exchange(grad_pre_bricks, send_list)
    sub_grad, received_g = lax.optimization_barrier((weight_grad(padded_x, grad_pre), received_g))
    table_g, _, _ = halo_table(grad_pre_bricks, received_g, cells)
    padded_g = pad_bricks(table_g, rows, voxels)
    grad_in = (conv_transpose(padded_g, w_sub) * occupancy[:, None]).astype(jnp.bfloat16)
    inverse_count = 1.0 / (lax.axis_size("space") * lax.axis_size("rep"))
    lanes = 128
    flat = jnp.concatenate([sub_grad.reshape(-1, lanes), down_grad.reshape(-1, lanes)])
    flat = joint_psum(flat, inverse_count)
    split = sub_grad.size // lanes
    sub_total = flat[:split].reshape(sub_grad.shape)
    down_total = flat[split:].reshape(down_grad.shape)
    return (
        coarse.reshape(1, bricks, voxels // 8, out_channels),
        grad_in.reshape(1, bricks, voxels, channels),
        sub_total,
        down_total.reshape(w_down.shape),
    )


def solution(mesh):
    in_specs = (
        P("rep", "space", None, None),
        P("rep", "space", None),
        P("rep", "space", None),
        P("rep", "space"),
        P(),
        P(),
        P("rep", "space", None, None),
    )
    out_specs = (P("rep", "space", None, None), P("rep", "space", None, None), P(), P())
    return jax.shard_map(body, mesh=mesh, in_specs=in_specs, out_specs=out_specs, check_vma=False)
```

```python
import jax
import numpy as np
import jax.numpy as jnp
from jax import lax
from jax.sharding import PartitionSpec as P


def from_behind(value, axis, steps):
    count = lax.axis_size(axis)
    leading, last = (max(0, -steps), min(count, count - steps))
    return lax.ppermute(value, axis, [(source, source + steps) for source in range(leading, last)])


HALVE = (None, (1, 4), (4, 16), (16, 1))
SPREAD = ((2, 8), (8, 32), (32, 64), (64, 2))


def joint_pairs(space_count, rep_count, masks):
    pairs = []
    for space in range(space_count):
        for rep in range(rep_count):
            if masks is None:
                target = space * rep_count + (rep ^ 1)
            else:
                target = (space ^ masks[rep]) * rep_count + rep
            pairs.append((space * rep_count + rep, target))
    return pairs


def step_bit(masks):
    rep = lax.axis_index("rep")
    if masks is None:
        return rep
    mask = jnp.where(rep == 0, masks[0], masks[1])
    return ((lax.axis_index("space") & mask) > 0).astype(jnp.int32)


def joint_psum(buf, scale):
    axes = ("space", "rep")
    counts = (lax.axis_size("space"), lax.axis_size("rep"))
    wide = buf.dtype
    for masks in HALVE:
        me = step_bit(masks)
        halves = buf.reshape(2, buf.shape[0] // 2, buf.shape[1])
        keep = lax.dynamic_index_in_dim(halves, me, 0, keepdims=False)
        send = lax.dynamic_index_in_dim(halves, 1 - me, 0, keepdims=False).astype(jnp.bfloat16)
        buf = keep + lax.ppermute(send, axes, joint_pairs(*counts, masks)).astype(wide)
    for masks in SPREAD:
        narrow = buf.astype(jnp.bfloat16)
        other = lax.ppermute(narrow, axes, joint_pairs(*counts, masks))
        buf = narrow.astype(wide) + other.astype(wide)
    buf = (buf * scale).astype(jnp.bfloat16)
    for masks in reversed(HALVE):
        me = step_bit(masks)
        other = lax.ppermute(buf, axes, joint_pairs(*counts, masks))
        buf = jnp.where(me == 0, jnp.concatenate([buf, other]), jnp.concatenate([other, buf]))
    return buf.astype(wide)


def padding_maps():
    side = np.array([0] + [1] * 8 + [2])
    inner = (np.arange(10) - 1) % 8
    column = side[:, None, None] * 9 + side[None, :, None] * 3 + side[None, None, :]
    voxel = inner[:, None, None] * 64 + inner[None, :, None] * 8 + inner[None, None, :]
    return column, voxel


def halo_exchange(values, send_list):
    bricks, voxels, channels = values.shape
    cells = send_list.shape[0]
    slot_row = jnp.zeros((1, channels), values.dtype).at[0, :cells].set(send_list.astype(values.dtype))
    payload = jnp.concatenate([values.reshape(bricks * voxels, channels), slot_row], axis=0)
    return from_behind(payload, "space", 1), from_behind(payload, "space", -1)


def halo_table(values, received, cells):
    bricks, voxels, channels = values.shape
    from_lower, from_upper = received
    block = bricks * voxels
    table = jnp.zeros(((3 * bricks + 1) * voxels, channels), values.dtype)
    table = lax.dynamic_update_slice(table, values.reshape(block, channels), (0, 0))
    table = lax.dynamic_update_slice(table, from_lower[:block], (block, 0))
    table = lax.dynamic_update_slice(table, from_upper[:block], (2 * block, 0))
    lower_slots = from_lower[bricks * voxels, :cells].astype(jnp.int32)
    upper_slots = from_upper[bricks * voxels, :cells].astype(jnp.int32)
    return table, lower_slots, upper_slots


def brick_rows(link_rows, lower_slots, upper_slots, bricks):
    cells = lower_slots.shape[0]
    empty = 3 * bricks
    lower = jnp.take(lower_slots, jnp.clip(link_rows - bricks, 0, cells - 1), mode="clip")
    upper = jnp.take(upper_slots, jnp.clip(link_rows - bricks - cells, 0, cells - 1), mode="clip")
    lower = jnp.where(lower < bricks, bricks + lower, empty)
    upper = jnp.where(upper < bricks, 2 * bricks + upper, empty)
    from_upper = jnp.where(link_rows < bricks + 2 * cells, upper, empty)
    from_side = jnp.where(link_rows < bricks + cells, lower, from_upper)
    return jnp.where(link_rows < bricks, link_rows, from_side)


def pad_bricks(table, rows, voxels):
    column, voxel = padding_maps()
    picks = jnp.asarray(column.reshape(1, -1, 1) == np.arange(rows.shape[1]).reshape(1, 1, -1))
    index = jnp.sum(jnp.where(picks, rows[:, None, :], 0), axis=-1) * voxels
    index = index + jnp.asarray(voxel.reshape(1, -1))
    padded = jnp.take(table, index.reshape(-1), axis=0, mode="clip")
    return padded.reshape(rows.shape[0], 10, 10, 10, table.shape[-1])


DIMS = ("NDHWC", "DHWIO", "NDHWC")


def conv_forward(padded, w_sub):
    channels = w_sub.shape[1]
    kernel = w_sub.reshape(3, 3, 3, channels, w_sub.shape[2])
    out = lax.conv_general_dilated(
        padded, kernel, (1, 1, 1), "VALID", dimension_numbers=DIMS,
        preferred_element_type=jnp.float32,
    )
    return out.reshape(-1, w_sub.shape[2])


def conv_transpose(padded, w_sub):
    kernel = w_sub.reshape(3, 3, 3, w_sub.shape[1], w_sub.shape[2])[::-1, ::-1, ::-1]
    kernel = kernel.transpose(0, 1, 2, 4, 3)
    out = lax.conv_general_dilated(
        padded, kernel, (1, 1, 1), "VALID", dimension_numbers=DIMS,
        preferred_element_type=jnp.float32,
    )
    return out.reshape(-1, w_sub.shape[1])


def weight_grad(padded, grad_rows):
    bricks = padded.shape[0]
    channels = padded.shape[-1]
    grads = grad_rows.reshape(bricks, 8, 8, 8, grad_rows.shape[-1])
    numbers = lax.ConvDimensionNumbers(
        lhs_spec=(4, 0, 1, 2, 3), rhs_spec=(4, 0, 1, 2, 3), out_spec=(3, 4, 0, 1, 2)
    )
    out = lax.conv_general_dilated(
        padded, grads, (1, 1, 1), "VALID", dimension_numbers=numbers,
        preferred_element_type=jnp.float32,
    )
    return out.reshape(27, channels, grad_rows.shape[-1])


def to_columns(values):
    bricks = values.shape[0]
    channels = values.shape[-1]
    cube = values.reshape(bricks, 4, 2, 4, 2, 4, 2, channels)
    return cube.transpose(0, 1, 3, 5, 2, 4, 6, 7).reshape(bricks * 64, 8 * channels)


def from_columns(columns, bricks, channels):
    cube = columns.reshape(bricks, 4, 4, 4, 2, 2, 2, channels)
    return cube.transpose(0, 1, 4, 2, 5, 3, 6, 7).reshape(bricks, 512, channels)


def silu_slope(values):
    sigmoid_value = jax.nn.sigmoid(values)
    return sigmoid_value * (1.0 + values * (1.0 - sigmoid_value))


def body(features, voxel_mask, neighbours, send_slots, w_sub, w_down, cotangent):
    values = features[0]
    bricks, voxels, channels = values.shape
    out_channels = w_down.shape[2]
    link_rows = neighbours[0]
    send_list = send_slots[0]
    occupancy = voxel_mask[0].reshape(-1).astype(jnp.float32)
    masked = values * voxel_mask[0][..., None].astype(jnp.bfloat16)
    cells = send_list.shape[0]
    table_x, lower_slots, upper_slots = halo_table(masked, halo_exchange(masked, send_list), cells)
    rows = brick_rows(link_rows, lower_slots, upper_slots, bricks)
    padded_x = pad_bricks(table_x, rows, voxels)
    pre_act = conv_forward(padded_x, w_sub) * occupancy[:, None]
    hidden = jax.nn.silu(pre_act).astype(jnp.bfloat16)
    columns = to_columns(hidden.reshape(bricks, voxels, channels))
    down_flat = w_down.reshape(-1, out_channels)
    coarse_mask = jnp.max(to_columns(occupancy.reshape(bricks, voxels, 1)), axis=1)
    coarse = (
        jnp.dot(columns, down_flat, preferred_element_type=jnp.float32) * coarse_mask[:, None]
    ).astype(jnp.bfloat16)
    grad_coarse = cotangent[0].reshape(-1, out_channels) * coarse_mask[:, None].astype(jnp.bfloat16)
    grad_cols = jnp.dot(grad_coarse, down_flat.T, preferred_element_type=jnp.float32).astype(
        jnp.bfloat16
    )
    grad_hidden = from_columns(grad_cols, bricks, channels).reshape(-1, channels)
    down_grad = lax.dot_general(
        columns, grad_coarse, (((0,), (0,)), ((), ())), preferred_element_type=jnp.float32
    )
    grad_pre = (grad_hidden.astype(jnp.float32) * silu_slope(pre_act) * occupancy[:, None]).astype(
        jnp.bfloat16
    )
    grad_pre_bricks = grad_pre.reshape(bricks, voxels, channels)
    received_g = halo_exchange(grad_pre_bricks, send_list)
    sub_grad, received_g = lax.optimization_barrier((weight_grad(padded_x, grad_pre), received_g))
    table_g, _, _ = halo_table(grad_pre_bricks, received_g, cells)
    padded_g = pad_bricks(table_g, rows, voxels)
    grad_in = (conv_transpose(padded_g, w_sub) * occupancy[:, None]).astype(jnp.bfloat16)
    inverse_count = 1.0 / (lax.axis_size("space") * lax.axis_size("rep"))
    lanes = 128
    flat = jnp.concatenate([sub_grad.reshape(-1, lanes), down_grad.reshape(-1, lanes)])
    flat = joint_psum(flat, inverse_count)
    split = sub_grad.size // lanes
    sub_total = flat[:split].reshape(sub_grad.shape)
    down_total = flat[split:].reshape(down_grad.shape)
    return (
        coarse.reshape(1, bricks, voxels // 8, out_channels),
        grad_in.reshape(1, bricks, voxels, channels),
        sub_total,
        down_total.reshape(w_down.shape),
    )


def solution(mesh):
    in_specs = (
        P("rep", "space", None, None),
        P("rep", "space", None),
        P("rep", "space", None),
        P("rep", "space"),
        P(),
        P(),
        P("rep", "space", None, None),
    )
    out_specs = (P("rep", "space", None, None), P("rep", "space", None, None), P(), P())
    return jax.shard_map(body, mesh=mesh, in_specs=in_specs, out_specs=out_specs, check_vma=False)
```

```python
import jax
import numpy as np
import jax.numpy as jnp
from jax import lax
from jax.sharding import PartitionSpec as P


def from_behind(value, axis, steps):
    count = lax.axis_size(axis)
    leading, last = (max(0, -steps), min(count, count - steps))
    return lax.ppermute(value, axis, [(source, source + steps) for source in range(leading, last)])


HALVE = (None, (1, 4), (4, 16), (16, 1))
SPREAD = ((2, 8), (8, 32), (32, 64), (64, 2))


def joint_pairs(space_count, rep_count, masks):
    pairs = []
    for space in range(space_count):
        for rep in range(rep_count):
            if masks is None:
                target = space * rep_count + (rep ^ 1)
            else:
                target = (space ^ masks[rep]) * rep_count + rep
            pairs.append((space * rep_count + rep, target))
    return pairs


def step_bit(masks):
    rep = lax.axis_index("rep")
    if masks is None:
        return rep
    mask = jnp.where(rep == 0, masks[0], masks[1])
    return ((lax.axis_index("space") & mask) > 0).astype(jnp.int32)


def joint_psum(buf, scale):
    axes = ("space", "rep")
    counts = (lax.axis_size("space"), lax.axis_size("rep"))
    wide = buf.dtype
    for masks in HALVE:
        me = step_bit(masks)
        halves = buf.reshape(2, buf.shape[0] // 2, buf.shape[1])
        keep = lax.dynamic_index_in_dim(halves, me, 0, keepdims=False)
        send = lax.dynamic_index_in_dim(halves, 1 - me, 0, keepdims=False).astype(jnp.bfloat16)
        buf = keep + lax.ppermute(send, axes, joint_pairs(*counts, masks)).astype(wide)
    for masks in SPREAD:
        narrow = buf.astype(jnp.bfloat16)
        other = lax.ppermute(narrow, axes, joint_pairs(*counts, masks))
        buf = narrow.astype(wide) + other.astype(wide)
    buf = (buf * scale).astype(jnp.bfloat16)
    for masks in reversed(HALVE):
        me = step_bit(masks)
        other = lax.ppermute(buf, axes, joint_pairs(*counts, masks))
        buf = jnp.where(me == 0, jnp.concatenate([buf, other]), jnp.concatenate([other, buf]))
    return buf.astype(wide)


def padding_maps():
    side = np.array([0] + [1] * 8 + [2])
    inner = (np.arange(10) - 1) % 8
    column = side[:, None, None] * 9 + side[None, :, None] * 3 + side[None, None, :]
    voxel = inner[:, None, None] * 64 + inner[None, :, None] * 8 + inner[None, None, :]
    return column, voxel


def halo_exchange(values, send_list):
    bricks, voxels, channels = values.shape
    cells = send_list.shape[0]
    slot_row = jnp.zeros((1, channels), values.dtype).at[0, :cells].set(send_list.astype(values.dtype))
    payload = jnp.concatenate([values.reshape(bricks * voxels, channels), slot_row], axis=0)
    return from_behind(payload, "space", 1), from_behind(payload, "space", -1)


def halo_table(values, received, cells):
    bricks, voxels, channels = values.shape
    from_lower, from_upper = received
    block = bricks * voxels
    table = jnp.zeros(((3 * bricks + 1) * voxels, channels), values.dtype)
    table = lax.dynamic_update_slice(table, values.reshape(block, channels), (0, 0))
    table = lax.dynamic_update_slice(table, from_lower[:block], (block, 0))
    table = lax.dynamic_update_slice(table, from_upper[:block], (2 * block, 0))
    lower_slots = from_lower[bricks * voxels, :cells].astype(jnp.int32)
    upper_slots = from_upper[bricks * voxels, :cells].astype(jnp.int32)
    return table, lower_slots, upper_slots


def brick_rows(link_rows, lower_slots, upper_slots, bricks):
    cells = lower_slots.shape[0]
    empty = 3 * bricks
    positions = jnp.arange(cells, dtype=jnp.int32)
    lower_hit = (link_rows - bricks)[..., None] == positions
    upper_hit = (link_rows - bricks - cells)[..., None] == positions
    lower = jnp.sum(jnp.where(lower_hit, lower_slots, 0), axis=-1)
    upper = jnp.sum(jnp.where(upper_hit, upper_slots, 0), axis=-1)
    lower = jnp.where(lower < bricks, bricks + lower, empty)
    upper = jnp.where(upper < bricks, 2 * bricks + upper, empty)
    from_upper = jnp.where(link_rows < bricks + 2 * cells, upper, empty)
    from_side = jnp.where(link_rows < bricks + cells, lower, from_upper)
    return jnp.where(link_rows < bricks, link_rows, from_side)


def pad_bricks(table, rows, voxels):
    column, voxel = padding_maps()
    picks = jnp.asarray(column.reshape(1, -1, 1) == np.arange(rows.shape[1]).reshape(1, 1, -1))
    index = jnp.sum(jnp.where(picks, rows[:, None, :], 0), axis=-1) * voxels
    index = index + jnp.asarray(voxel.reshape(1, -1))
    padded = jnp.take(table, index.reshape(-1), axis=0, mode="clip")
    return padded.reshape(rows.shape[0], 10, 10, 10, table.shape[-1])


DIMS = ("NDHWC", "DHWIO", "NDHWC")


def conv_forward(padded, w_sub):
    channels = w_sub.shape[1]
    kernel = w_sub.reshape(3, 3, 3, channels, w_sub.shape[2])
    out = lax.conv_general_dilated(
        padded, kernel, (1, 1, 1), "VALID", dimension_numbers=DIMS,
        preferred_element_type=jnp.float32,
    )
    return out.reshape(-1, w_sub.shape[2])


def conv_transpose(padded, w_sub):
    kernel = w_sub.reshape(3, 3, 3, w_sub.shape[1], w_sub.shape[2])[::-1, ::-1, ::-1]
    kernel = kernel.transpose(0, 1, 2, 4, 3)
    out = lax.conv_general_dilated(
        padded, kernel, (1, 1, 1), "VALID", dimension_numbers=DIMS,
        preferred_element_type=jnp.float32,
    )
    return out.reshape(-1, w_sub.shape[1])


def weight_grad(padded, grad_rows):
    bricks = padded.shape[0]
    channels = padded.shape[-1]
    grads = grad_rows.reshape(bricks, 8, 8, 8, grad_rows.shape[-1])
    numbers = lax.ConvDimensionNumbers(
        lhs_spec=(4, 0, 1, 2, 3), rhs_spec=(4, 0, 1, 2, 3), out_spec=(3, 4, 0, 1, 2)
    )
    out = lax.conv_general_dilated(
        padded, grads, (1, 1, 1), "VALID", dimension_numbers=numbers,
        preferred_element_type=jnp.float32,
    )
    return out.reshape(27, channels, grad_rows.shape[-1])


def to_columns(values):
    bricks = values.shape[0]
    channels = values.shape[-1]
    cube = values.reshape(bricks, 4, 2, 4, 2, 4, 2, channels)
    return cube.transpose(0, 1, 3, 5, 2, 4, 6, 7).reshape(bricks * 64, 8 * channels)


def from_columns(columns, bricks, channels):
    cube = columns.reshape(bricks, 4, 4, 4, 2, 2, 2, channels)
    return cube.transpose(0, 1, 4, 2, 5, 3, 6, 7).reshape(bricks, 512, channels)


def silu_slope(values):
    sigmoid_value = jax.nn.sigmoid(values)
    return sigmoid_value * (1.0 + values * (1.0 - sigmoid_value))


def body(features, voxel_mask, neighbours, send_slots, w_sub, w_down, cotangent):
    values = features[0]
    bricks, voxels, channels = values.shape
    out_channels = w_down.shape[2]
    link_rows = neighbours[0]
    send_list = send_slots[0]
    occupancy = voxel_mask[0].reshape(-1).astype(jnp.float32)
    masked = values * voxel_mask[0][..., None].astype(jnp.bfloat16)
    cells = send_list.shape[0]
    table_x, lower_slots, upper_slots = halo_table(masked, halo_exchange(masked, send_list), cells)
    rows = brick_rows(link_rows, lower_slots, upper_slots, bricks)
    padded_x = pad_bricks(table_x, rows, voxels)
    pre_act = conv_forward(padded_x, w_sub) * occupancy[:, None]
    hidden = jax.nn.silu(pre_act).astype(jnp.bfloat16)
    columns = to_columns(hidden.reshape(bricks, voxels, channels))
    down_flat = w_down.reshape(-1, out_channels)
    coarse_mask = jnp.max(to_columns(occupancy.reshape(bricks, voxels, 1)), axis=1)
    coarse = (
        jnp.dot(columns, down_flat, preferred_element_type=jnp.float32) * coarse_mask[:, None]
    ).astype(jnp.bfloat16)
    grad_coarse = cotangent[0].reshape(-1, out_channels) * coarse_mask[:, None].astype(jnp.bfloat16)
    grad_cols = jnp.dot(grad_coarse, down_flat.T, preferred_element_type=jnp.float32).astype(
        jnp.bfloat16
    )
    grad_hidden = from_columns(grad_cols, bricks, channels).reshape(-1, channels)
    down_grad = lax.dot_general(
        columns, grad_coarse, (((0,), (0,)), ((), ())), preferred_element_type=jnp.float32
    )
    grad_pre = (grad_hidden.astype(jnp.float32) * silu_slope(pre_act) * occupancy[:, None]).astype(
        jnp.bfloat16
    )
    grad_pre_bricks = grad_pre.reshape(bricks, voxels, channels)
    received_g = halo_exchange(grad_pre_bricks, send_list)
    sub_grad, received_g = lax.optimization_barrier((weight_grad(padded_x, grad_pre), received_g))
    table_g, _, _ = halo_table(grad_pre_bricks, received_g, cells)
    padded_g = pad_bricks(table_g, rows, voxels)
    grad_in = (conv_transpose(padded_g, w_sub) * occupancy[:, None]).astype(jnp.bfloat16)
    inverse_count = 1.0 / (lax.axis_size("space") * lax.axis_size("rep"))
    lanes = 128
    flat = jnp.concatenate([sub_grad.reshape(-1, lanes), down_grad.reshape(-1, lanes)])
    flat = joint_psum(flat, inverse_count)
    split = sub_grad.size // lanes
    sub_total = flat[:split].reshape(sub_grad.shape)
    down_total = flat[split:].reshape(down_grad.shape)
    return (
        coarse.reshape(1, bricks, voxels // 8, out_channels),
        grad_in.reshape(1, bricks, voxels, channels),
        sub_total,
        down_total.reshape(w_down.shape),
    )


def solution(mesh):
    in_specs = (
        P("rep", "space", None, None),
        P("rep", "space", None),
        P("rep", "space", None),
        P("rep", "space"),
        P(),
        P(),
        P("rep", "space", None, None),
    )
    out_specs = (P("rep", "space", None, None), P("rep", "space", None, None), P(), P())
    return jax.shard_map(body, mesh=mesh, in_specs=in_specs, out_specs=out_specs, check_vma=False)
```
